256 devices in a mesh: dom: 32 (over x, z), head: 8 (over y, core).
Axes of the slice: x: 4, y: 4, z: 8, core: 2. Of those that a mesh axis runs over, the one named last changes fastest.
Arguments:
- features: bfloat16 [131072, 512], P(('dom', 'head')), may hold values from -6 to 6
- norm_gain: float32 [512], replicated, may hold values from 0.5 to 1.5
- w_qkv: bfloat16 [512, 1536], replicated, may hold values from -8 to 8
- w_out: bfloat16 [512, 512], replicated, may hold values from -0.25 to 0.25
- grad_y: bfloat16 [131072, 512], P(('dom', 'head')), may hold values from -6 to 6
- local_keys: int32 [1024, 4], P('dom'), may hold values from 0 to 31, as said below
- remote_keys: int32 [1024, 4], P('dom'), may hold values from 0 to 95
- boundary_blocks: int32 [32, 32, 3], P('dom'), may hold values from 0 to 31
- boundary_count: int32 [32, 32], P(None, 'dom'), may hold values from 1 to 3
Outputs:
- mixed_out: bfloat16 [131072, 512], P(('dom', 'head'))
- grad_x: bfloat16 [131072, 512], P(('dom', 'head'))
The draws below stay inside these ranges and needn't reach their ends.
Inputs may be any that keep to these rules, and one draw needn't show every extreme that they name: `local_keys`: column 0 of row b is b % 32, the query block itself.
All inputs are finite; a program needn't handle non-finite values.
Results may differ from the reference program's by a relative error of at most 0.012.
The reference program's roundings to bfloat16 on the way count: a program that leaves them out, or rounds other values in their place, can miss the bound.
Values may be sent and summed in bfloat16 or wider, within the bound.
No kernel may reach another device: no remote copies, remote signals or barrier semaphores. Data moves between devices by JAX's collectives and lax.ppermute only.
A program may use at most 128 MiB of HBM per device.

```python
import jax
import jax.numpy as jnp
from jax import lax

D = 512
HEADS = 8
DH = 64
BS = 128
KL = 4
KR = 4
BPAIR = 3
GBLK = 32
NBLK = 1024
NODES = 131072
SLOTS = 96
N_DOM = 32


def draw_w_qkv(key, part):
    first = jax.random.fold_in(key, 0)
    base = jax.random.normal(first, (D, 3 * D), jnp.float32) * D ** (-0.5)
    query_cols = base[:, :D] * 2.0
    value_cols = base[:, 2 * D:]
    key_cols = base[:, D:2 * D] * 2.0
    whole = jnp.concatenate([query_cols, key_cols, value_cols], axis=1)
    return jnp.clip(whole, -8.0, 8.0).astype(jnp.bfloat16)


def draw_local_keys(key, part):
    own = jnp.arange(NBLK, dtype=jnp.int32) % GBLK
    others = jax.random.randint(key, (NBLK, KL - 1), 0, GBLK, dtype=jnp.int32)
    return jnp.concatenate([own[:, None], others], axis=1)


def plant(result, rng, smallest, top_value):
    extent = result.shape
    place = [jax.random.randint(jax.random.fold_in(rng, axis), (), 0, extent[axis]) for axis in range(len(extent))]
    result = result.at[tuple(place)].set(smallest)
    longest = extent.index(max(extent))
    place[longest] = (place[longest] + 1) % extent[longest]
    return result.at[tuple(place)].set(top_value)


def level_of(rng, extent, cuts, low, top_value):
    def one(axis_at, parts):
        heights = jax.random.uniform(jax.random.fold_in(jax.random.fold_in(rng, 6), axis_at), (parts,), jnp.float32, low / len(cuts), top_value / len(cuts))
        return jnp.repeat(jnp.exp(heights), extent[axis_at] // parts).reshape((-1,) + (1,) * (len(extent) - axis_at - 1))

    level = one(*cuts[0])
    for cut in cuts[1:]:
        level = level * one(*cut)
    return level


def bell_draw(own_key, extent, spread, limit, shards=(), kind=jnp.bfloat16):
    values = spread * jax.random.normal(own_key, extent, jnp.float32)
    if shards:
        values = values * level_of(own_key, extent, shards, -0.22, 0.18)
    return jnp.clip(values, -limit, limit).astype(kind)


def setup_inputs(seed: int = 0) -> dict:
    splits = jax.random.split(jax.random.key(seed), 10)
    features = bell_draw(splits[0], (NODES, D), 1.0, 6.0, ((0, 256),))
    norm_gain = jnp.clip(1.0 + 0.1 * jax.random.normal(splits[1], (D,), jnp.float32), 0.5, 1.5)
    w_qkv = draw_w_qkv(jax.random.fold_in(splits[9], 71), 0)
    w_out = bell_draw(splits[3], (D, D), D ** -0.5, 0.25)
    grad_y = bell_draw(splits[4], (NODES, D), 1.0, 6.0, ((0, 256),))
    local_keys = draw_local_keys(jax.random.fold_in(splits[9], 71), 0)
    remote_keys = plant(jax.random.randint(splits[6], (NBLK, KR), 0, SLOTS), jax.random.fold_in(splits[6], 1), 0, SLOTS - 1).astype(jnp.int32)
    boundary_blocks = plant(jax.random.randint(splits[7], (N_DOM, N_DOM, BPAIR), 0, GBLK), jax.random.fold_in(splits[7], 1), 0, GBLK - 1).astype(jnp.int32)
    boundary_count = plant(jax.random.randint(splits[8], (N_DOM, N_DOM), 1, BPAIR + 1), jax.random.fold_in(splits[8], 1), 1, BPAIR).astype(jnp.int32)
    return {"features": features, "norm_gain": norm_gain, "w_qkv": w_qkv, "w_out": w_out, "grad_y": grad_y, "local_keys": local_keys, "remote_keys": remote_keys, "boundary_blocks": boundary_blocks, "boundary_count": boundary_count}


EPS = 1e-05

def rounded(value):
    return lax.optimization_barrier(value.astype(jnp.bfloat16))

def probabilities(queries, keys, alive, score_scale):
    scores = jnp.einsum('qbpe,qkcpe->qbpkc', queries.astype(jnp.float32), keys.astype(jnp.float32)) * score_scale
    masked = jnp.where(alive[:, None, None, :, None], scores, -jnp.inf)
    top = lax.optimization_barrier(jnp.max(masked, axis=(3, 4), keepdims=True))
    expo = jnp.exp(masked - top)
    total = lax.optimization_barrier(jnp.sum(expo, axis=(3, 4), keepdims=True))
    return rounded(expo / total)

def reference(features, norm_gain, w_qkv, w_out, grad_y, local_keys, remote_keys, boundary_blocks, boundary_count):
    f32 = jnp.float32
    score_scale = DH ** (-0.5)
    xf = features.astype(f32)
    inv = lax.rsqrt(lax.optimization_barrier(jnp.mean(xf * xf, axis=1, keepdims=True)) + EPS)
    normed = xf * inv
    hidden = rounded(normed * norm_gain)
    qkv = rounded(jnp.dot(hidden, w_qkv, preferred_element_type=f32)).reshape(NBLK, BS, 3, HEADS * DH)
    queries = qkv[:, :, 0].reshape(N_DOM, GBLK, BS, HEADS, DH)
    kv_blocks = qkv[:, :, 1:].reshape(NBLK, BS * 2 * HEADS * DH)
    slot = jnp.arange(SLOTS, dtype=jnp.int32)
    source = slot // BPAIR
    position = slot % BPAIR
    target = jnp.arange(N_DOM, dtype=jnp.int32)[:, None]
    slot_block = (source[None, :] * GBLK + boundary_blocks[source[None, :], target, position[None, :]]).astype(jnp.int32)
    slot_alive = position[None, :] < boundary_count[source[None, :], target]
    group_base = (jnp.arange(N_DOM, dtype=jnp.int32) * GBLK)[:, None, None]
    local_ids = (local_keys.reshape(N_DOM, GBLK, KL) + group_base).astype(jnp.int32)
    remote_local = remote_keys.reshape(N_DOM, GBLK, KR).astype(jnp.int32)
    remote_ids = jax.vmap(lambda table, picks: table[picks])(slot_block, remote_local)
    remote_alive = jax.vmap(lambda table, picks: table[picks])(slot_alive, remote_local)
    all_ids = jnp.concatenate([local_ids, remote_ids], axis=2).astype(jnp.int32)

    def gather_keys(ids, alive_far):
        both = jnp.take(kv_blocks, ids, axis=0).reshape(GBLK, KL + KR, BS, 2, HEADS, DH)
        alive = jnp.concatenate([jnp.ones((GBLK, KL), jnp.bool_), alive_far], axis=1)
        return (both[:, :, :, 0], both[:, :, :, 1], alive)

    def forward(item):
        query_part, ids, alive_far = item
        keys, values, alive = gather_keys(ids, alive_far)
        weights = probabilities(query_part, keys, alive, score_scale)
        return rounded(jnp.einsum('qbpkc,qkcpe->qbpe', weights.astype(f32), values.astype(f32)))
    outs = lax.map(forward, (queries, all_ids, remote_alive))
    attn = outs.reshape(NODES, D)
    mixed_out = (xf + jnp.dot(attn, w_out, preferred_element_type=f32)).astype(jnp.bfloat16)
    d_attn = rounded(jnp.dot(grad_y, w_out.T, preferred_element_type=f32)).reshape(N_DOM, GBLK, BS, HEADS, DH)
    flat = BS * 2 * HEADS * DH

    def backward(carry, item):
        query_part, ids, alive_far, slot_ids, remote_part, d_out, out_part = item
        keys, values, alive = gather_keys(ids, alive_far)
        weights = probabilities(query_part, keys, alive, score_scale)
        d_outf = d_out.astype(f32)
        delta = lax.optimization_barrier(jnp.sum(d_outf * out_part.astype(f32), axis=-1))
        d_weights = jnp.einsum('qbpe,qkcpe->qbpkc', d_outf, values.astype(f32))
        d_scores = rounded(weights.astype(f32) * (d_weights - delta[:, :, :, None, None]) * score_scale).astype(f32)
        d_query = jnp.einsum('qbpkc,qkcpe->qbpe', d_scores, keys.astype(f32))
        d_key = jnp.einsum('qbpkc,qbpe->qkcpe', d_scores, query_part.astype(f32))
        d_value = jnp.einsum('qbpkc,qbpe->qkcpe', weights.astype(f32), d_outf)
        d_pair = jnp.stack([d_key, d_value], axis=3).reshape(GBLK, KL + KR, flat)
        carry = carry.at[ids[:, :KL].reshape(-1)].add(d_pair[:, :KL].reshape(-1, flat))
        slot_sum = jnp.zeros((SLOTS, flat), f32).at[remote_part.reshape(-1)].add(d_pair[:, KL:].reshape(-1, flat))
        carry = carry.at[slot_ids].add(rounded(slot_sum).astype(f32))
        return (carry, d_query)
    items = (queries, all_ids, remote_alive, slot_block, remote_local, d_attn, outs)
    carry, d_queries = lax.scan(backward, jnp.zeros((NBLK, flat), f32), items)
    d_kv = carry.reshape(NBLK, BS, 2, HEADS * DH)
    d_q = d_queries.reshape(NBLK, BS, 1, HEADS * DH)
    d_qkv = rounded(jnp.concatenate([d_q, d_kv], axis=2)).reshape(NODES, 3 * D)
    d_hidden = jnp.dot(d_qkv, w_qkv.T, preferred_element_type=f32)
    d_normed = d_hidden * norm_gain
    d_input = inv * (d_normed - normed * lax.optimization_barrier(jnp.mean(d_normed * normed, axis=1, keepdims=True)))
    grad_x = (grad_y.astype(f32) + d_input).astype(jnp.bfloat16)
    return (mixed_out, grad_x)
```

```python
import math

import jax
import jax.numpy as jnp
from jax import lax
from jax.experimental import pallas as pl
from jax.experimental.pallas import tpu as pltpu
from jax.sharding import PartitionSpec as P

HEADS = 8
EPS = 1e-05


def attention_kernel(
    lk_ref, rk_ref, q_ref, do_ref, kl_ref, vl_ref, kp_ref, vp_ref, bias_ref,
    o_ref, dq_ref, dkl_ref, dvl_ref, dkp_ref, dvp_ref, *, near, far, bsize, scale
):
    f32 = jnp.float32
    bf16 = jnp.bfloat16
    nq = q_ref.shape[0]
    dkl_ref[...] = jnp.zeros(dkl_ref.shape, f32)
    dvl_ref[...] = jnp.zeros(dvl_ref.shape, f32)
    dkp_ref[...] = jnp.zeros(dkp_ref.shape, f32)
    dvp_ref[...] = jnp.zeros(dvp_ref.shape, f32)

    def body(b, carry):
        q = q_ref[b]
        do = do_ref[b]
        ids_l = [lk_ref[b * near + i] for i in range(near)]
        ids_r = [rk_ref[b * far + i] for i in range(far)]
        keys = jnp.concatenate([kl_ref[i] for i in ids_l] + [kp_ref[i] for i in ids_r], axis=0)
        vals = jnp.concatenate([vl_ref[i] for i in ids_l] + [vp_ref[i] for i in ids_r], axis=0)
        s = lax.dot_general(q, keys, (((1,), (1,)), ((), ())), preferred_element_type=f32) * scale
        s = s + bias_ref[b]
        top = jnp.max(s, axis=1, keepdims=True)
        expo = jnp.exp(s - top)
        total = jnp.sum(expo, axis=1, keepdims=True)
        w = (expo / total).astype(bf16)
        o = jnp.dot(w, vals, preferred_element_type=f32).astype(bf16)
        o_ref[b] = o
        delta = jnp.sum(do.astype(f32) * o.astype(f32), axis=1, keepdims=True)
        dw = lax.dot_general(do, vals, (((1,), (1,)), ((), ())), preferred_element_type=f32)
        ds = (w.astype(f32) * (dw - delta) * scale).astype(bf16)
        dq_ref[b] = jnp.dot(ds, keys, preferred_element_type=f32)
        dk = lax.dot_general(ds, q, (((0,), (0,)), ((), ())), preferred_element_type=f32)
        dv = lax.dot_general(w, do, (((0,), (0,)), ((), ())), preferred_element_type=f32)
        for i in range(near):
            part = slice(i * bsize, (i + 1) * bsize)
            dkl_ref[ids_l[i]] = dkl_ref[ids_l[i]] + dk[part]
            dvl_ref[ids_l[i]] = dvl_ref[ids_l[i]] + dv[part]
        for i in range(far):
            part = slice((near + i) * bsize, (near + i + 1) * bsize)
            dkp_ref[ids_r[i]] = dkp_ref[ids_r[i]] + dk[part]
            dvp_ref[ids_r[i]] = dvp_ref[ids_r[i]] + dv[part]
        return carry

    lax.fori_loop(0, nq, body, 0)


def fused_attention(local_ids, remote_ids, q, d_out, k_loc, v_loc, k_pool, v_pool, bias, scale):
    nq, bsize, depth = q.shape
    near = local_ids.size // nq
    far = remote_ids.size // nq
    nloc = k_loc.shape[0]
    npool = k_pool.shape[0]
    f32 = jnp.float32
    smem = pl.BlockSpec(memory_space=pltpu.SMEM)
    vmem = pl.BlockSpec(memory_space=pltpu.VMEM)
    kernel = lambda *refs: attention_kernel(
        *refs, near=near, far=far, bsize=bsize, scale=scale
    )
    return pl.pallas_call(
        kernel,
        out_shape=(
            jax.ShapeDtypeStruct((nq, bsize, depth), jnp.bfloat16),
            jax.ShapeDtypeStruct((nq, bsize, depth), f32),
            jax.ShapeDtypeStruct((nloc, bsize, depth), f32),
            jax.ShapeDtypeStruct((nloc, bsize, depth), f32),
            jax.ShapeDtypeStruct((npool, bsize, depth), f32),
            jax.ShapeDtypeStruct((npool, bsize, depth), f32),
        ),
        in_specs=[smem, smem] + [vmem] * 7,
        out_specs=tuple([vmem] * 6),
        compiler_params=pltpu.CompilerParams(vmem_limit_bytes=60 * 1024 * 1024),
    )(local_ids, remote_ids, q, d_out, k_loc, v_loc, k_pool, v_pool, bias)


def local(
    features,
    norm_gain,
    w_qkv,
    w_out,
    grad_y,
    local_keys,
    remote_keys,
    boundary_blocks,
    boundary_count,
):
    f32 = jnp.float32
    bf16 = jnp.bfloat16
    nhead = lax.axis_size("head")
    rows, width = features.shape
    per = HEADS // nhead
    depth = width // HEADS
    hwide = per * depth
    nblk, near_count = local_keys.shape
    far_count = remote_keys.shape[1]
    ndom = boundary_blocks.shape[1]
    pair_slots = boundary_blocks.shape[2]
    slots = ndom * pair_slots
    grows = rows * nhead
    bsize = grows // nblk
    score_scale = 1.0 / math.sqrt(depth)

    xf = features.astype(f32)
    inv = lax.rsqrt(jnp.mean(xf * xf, axis=1, keepdims=True) + EPS)
    normed = xf * inv
    hidden = (normed * norm_gain).astype(bf16)
    w_heads = (
        w_qkv.reshape(width, 3, nhead, hwide).transpose(0, 2, 1, 3).reshape(width, 3 * width)
    )
    qkv_own = jnp.dot(hidden, w_heads, preferred_element_type=f32).astype(bf16)
    qkv = lax.all_to_all(
        qkv_own.reshape(rows, nhead, 3 * hwide), "head", split_axis=1, concat_axis=0, tiled=True
    ).reshape(nblk, bsize, 3, hwide)
    queries = qkv[:, :, 0]
    kv_blocks = qkv[:, :, 1:]

    d_attn = jnp.dot(grad_y, w_out.T, preferred_element_type=f32).astype(bf16)
    d_group = lax.all_to_all(
        d_attn.reshape(rows, nhead, hwide), "head", split_axis=1, concat_axis=0, tiled=True
    ).reshape(nblk, bsize, hwide)

    send_ids = boundary_blocks[0]
    outgoing = jnp.take(kv_blocks, send_ids.reshape(-1), axis=0)
    pool = lax.all_to_all(
        outgoing.reshape(ndom, pair_slots, bsize, 2, hwide),
        "dom",
        split_axis=0,
        concat_axis=0,
        tiled=True,
    ).reshape(slots, bsize, 2, hwide)
    slot_alive = (jnp.arange(pair_slots, dtype=jnp.int32)[None, :] < boundary_count).reshape(slots)
    remote_alive = jnp.take(slot_alive, remote_keys, axis=0)
    bias_far = jnp.where(remote_alive, 0.0, -jnp.inf).astype(f32)
    bias = jnp.concatenate(
        [jnp.zeros((nblk, near_count), f32), bias_far], axis=1
    )
    bias = jnp.repeat(bias, bsize, axis=1).reshape(nblk, 1, (near_count + far_count) * bsize)

    o, d_q, dk_loc, dv_loc, dk_pool, dv_pool = fused_attention(
        local_keys.reshape(-1),
        remote_keys.reshape(-1),
        queries,
        d_group,
        kv_blocks[:, :, 0],
        kv_blocks[:, :, 1],
        pool[:, :, 0],
        pool[:, :, 1],
        bias,
        score_scale,
    )

    attn = lax.all_to_all(
        o.reshape(grows, hwide), "head", split_axis=0, concat_axis=1, tiled=True
    )
    mixed_out = (xf + jnp.dot(attn, w_out, preferred_element_type=f32)).astype(bf16)

    slot_grads = jnp.stack([dk_pool, dv_pool], axis=2).astype(bf16)
    returned = lax.all_to_all(
        slot_grads.reshape(ndom, pair_slots, bsize * 2 * hwide),
        "dom",
        split_axis=0,
        concat_axis=0,
        tiled=True,
    ).reshape(slots, bsize * 2 * hwide)
    onehot = (
        send_ids.reshape(1, slots) == jnp.arange(nblk, dtype=jnp.int32)[:, None]
    ).astype(bf16)
    d_kv = jnp.stack([dk_loc, dv_loc], axis=2).reshape(nblk, bsize * 2 * hwide) + jnp.dot(
        onehot, returned, preferred_element_type=f32
    )
    d_qkv = jnp.concatenate(
        [d_q.reshape(nblk, bsize, 1, hwide), d_kv.reshape(nblk, bsize, 2, hwide)], axis=2
    ).astype(bf16)
    d_rows = lax.all_to_all(
        d_qkv.reshape(grows, 3 * hwide), "head", split_axis=0, concat_axis=1, tiled=True
    )
    d_hidden = jnp.dot(d_rows, w_heads.T, preferred_element_type=f32)
    d_normed = d_hidden * norm_gain
    d_input = inv * (d_normed - normed * jnp.mean(d_normed * normed, axis=1, keepdims=True))
    grad_x = (grad_y.astype(f32) + d_input).astype(bf16)
    return (mixed_out, grad_x)


def solution(mesh):
    return jax.shard_map(
        local,
        mesh=mesh,
        in_specs=(
            P(("dom", "head"), None),
            P(),
            P(),
            P(),
            P(("dom", "head"), None),
            P("dom", None),
            P("dom", None),
            P("dom", None, None),
            P(None, "dom"),
        ),
        out_specs=(P(("dom", "head"), None), P(("dom", "head"), None)),
        check_vma=False,
    )
```

```python
import math

import jax
import jax.numpy as jnp
from jax import lax
from jax.experimental import pallas as pl
from jax.experimental.pallas import tpu as pltpu
from jax.sharding import PartitionSpec as P

HEADS = 8
EPS = 1e-05


def attention_kernel(
    lk_ref, rk_ref, qkv_ref, do_ref, pool_ref, bias_ref, o_ref, acc_ref, slot_ref, slot_acc,
    *, near, far, bsize, depth, scale
):
    f32 = jnp.float32
    bf16 = jnp.bfloat16
    nq = qkv_ref.shape[0]
    acc_ref[...] = jnp.zeros(acc_ref.shape, f32)
    slot_acc[...] = jnp.zeros(slot_acc.shape, f32)
    kcols = pl.ds(depth, depth)
    vcols = pl.ds(2 * depth, depth)
    pk = pl.ds(0, depth)
    pv = pl.ds(depth, depth)

    def body(b, carry):
        q = qkv_ref[b, :, pl.ds(0, depth)]
        do = do_ref[b]
        ids_l = [lk_ref[b * near + i] for i in range(near)]
        ids_r = [rk_ref[b * far + i] for i in range(far)]
        keys = jnp.concatenate(
            [qkv_ref[i, :, kcols] for i in ids_l] + [pool_ref[i, :, pk] for i in ids_r], axis=0
        )
        vals = jnp.concatenate(
            [qkv_ref[i, :, vcols] for i in ids_l] + [pool_ref[i, :, pv] for i in ids_r], axis=0
        )
        s = lax.dot_general(q, keys, (((1,), (1,)), ((), ())), preferred_element_type=f32) * scale
        s = s + bias_ref[b]
        top = jnp.max(s, axis=1, keepdims=True)
        expo = jnp.exp(s - top)
        total = jnp.sum(expo, axis=1, keepdims=True)
        w = (expo / total).astype(bf16)
        o = jnp.dot(w, vals, preferred_element_type=f32).astype(bf16)
        o_ref[b] = o
        delta = jnp.sum(do.astype(f32) * o.astype(f32), axis=1, keepdims=True)
        dw = lax.dot_general(do, vals, (((1,), (1,)), ((), ())), preferred_element_type=f32)
        ds = (w.astype(f32) * (dw - delta) * scale).astype(bf16)
        acc_ref[b, :, pl.ds(0, depth)] = jnp.dot(ds, keys, preferred_element_type=f32)
        dk = lax.dot_general(ds, q, (((0,), (0,)), ((), ())), preferred_element_type=f32)
        dv = lax.dot_general(w, do, (((0,), (0,)), ((), ())), preferred_element_type=f32)
        for i in range(near):
            part = slice(i * bsize, (i + 1) * bsize)
            acc_ref[ids_l[i], :, kcols] = acc_ref[ids_l[i], :, kcols] + dk[part]
            acc_ref[ids_l[i], :, vcols] = acc_ref[ids_l[i], :, vcols] + dv[part]
        for i in range(far):
            part = slice((near + i) * bsize, (near + i + 1) * bsize)
            slot_acc[ids_r[i], :, pk] = slot_acc[ids_r[i], :, pk] + dk[part]
            slot_acc[ids_r[i], :, pv] = slot_acc[ids_r[i], :, pv] + dv[part]
        return carry

    lax.fori_loop(0, nq, body, 0)
    slot_ref[...] = slot_acc[...].astype(bf16)


def fused_attention(local_ids, remote_ids, qkv, d_out, pool, bias, scale):
    nq, bsize, depth = d_out.shape
    near = local_ids.size // nq
    far = remote_ids.size // nq
    npool = pool.shape[0]
    f32 = jnp.float32
    smem = pl.BlockSpec(memory_space=pltpu.SMEM)
    vmem = pl.BlockSpec(memory_space=pltpu.VMEM)
    kernel = lambda *refs: attention_kernel(
        *refs, near=near, far=far, bsize=bsize, depth=depth, scale=scale
    )
    return pl.pallas_call(
        kernel,
        out_shape=(
            jax.ShapeDtypeStruct((nq, bsize, depth), jnp.bfloat16),
            jax.ShapeDtypeStruct(qkv.shape, f32),
            jax.ShapeDtypeStruct(pool.shape, jnp.bfloat16),
        ),
        in_specs=[smem, smem] + [vmem] * 4,
        out_specs=(vmem, vmem, vmem),
        scratch_shapes=[pltpu.VMEM(pool.shape, f32)],
        compiler_params=pltpu.CompilerParams(vmem_limit_bytes=60 * 1024 * 1024),
    )(local_ids, remote_ids, qkv, d_out, pool, bias)


def finish_kernel(ids_ref, acc_ref, ret_ref, out_ref, total_ref, *, depth):
    width = ret_ref.shape[2]
    total_ref[...] = acc_ref[...]

    def body(j, carry):
        i = ids_ref[j]
        cols = pl.ds(depth, width)
        total_ref[i, :, cols] = total_ref[i, :, cols] + ret_ref[j].astype(jnp.float32)
        return carry

    lax.fori_loop(0, ret_ref.shape[0], body, 0)
    out_ref[...] = total_ref[...].astype(jnp.bfloat16)


def finish_grads(send_ids, acc, returned, depth):
    smem = pl.BlockSpec(memory_space=pltpu.SMEM)
    vmem = pl.BlockSpec(memory_space=pltpu.VMEM)
    return pl.pallas_call(
        lambda *refs: finish_kernel(*refs, depth=depth),
        out_shape=jax.ShapeDtypeStruct(acc.shape, jnp.bfloat16),
        in_specs=[smem, vmem, vmem],
        out_specs=vmem,
        scratch_shapes=[pltpu.VMEM(acc.shape, jnp.float32)],
        compiler_params=pltpu.CompilerParams(vmem_limit_bytes=60 * 1024 * 1024),
    )(send_ids, acc, returned)


def local(
    features,
    norm_gain,
    w_qkv,
    w_out,
    grad_y,
    local_keys,
    remote_keys,
    boundary_blocks,
    boundary_count,
):
    f32 = jnp.float32
    bf16 = jnp.bfloat16
    nhead = lax.axis_size("head")
    rows, width = features.shape
    per = HEADS // nhead
    depth = width // HEADS
    hwide = per * depth
    nblk, near_count = local_keys.shape
    far_count = remote_keys.shape[1]
    ndom = boundary_blocks.shape[1]
    pair_slots = boundary_blocks.shape[2]
    slots = ndom * pair_slots
    grows = rows * nhead
    bsize = grows // nblk
    score_scale = 1.0 / math.sqrt(depth)

    xf = features.astype(f32)
    inv = lax.rsqrt(jnp.mean(xf * xf, axis=1, keepdims=True) + EPS)
    normed = xf * inv
    hidden = (normed * norm_gain).astype(bf16)
    w_heads = (
        w_qkv.reshape(width, 3, nhead, hwide).transpose(2, 0, 1, 3).reshape(nhead, width, 3 * hwide)
    )
    w_out_heads = w_out.reshape(nhead, hwide, width)
    qkv_own = jnp.einsum("rd,hdc->hrc", hidden, w_heads, preferred_element_type=f32).astype(bf16)
    qkv = lax.all_to_all(qkv_own, "head", split_axis=0, concat_axis=0, tiled=True).reshape(
        nblk, bsize, 3 * hwide
    )

    d_attn = jnp.einsum("rf,hef->hre", grad_y, w_out_heads, preferred_element_type=f32).astype(bf16)
    d_group = lax.all_to_all(d_attn, "head", split_axis=0, concat_axis=0, tiled=True).reshape(
        nblk, bsize, hwide
    )

    send_ids = boundary_blocks[0].reshape(slots)
    outgoing = jnp.take(qkv[:, :, hwide:], send_ids, axis=0)
    pool = lax.all_to_all(
        outgoing.reshape(ndom, pair_slots * bsize, 2 * hwide),
        "dom",
        split_axis=0,
        concat_axis=0,
        tiled=True,
    ).reshape(slots, bsize, 2 * hwide)
    slot_alive = (jnp.arange(pair_slots, dtype=jnp.int32)[None, :] < boundary_count).reshape(slots)
    remote_alive = jnp.take(slot_alive, remote_keys, axis=0)
    bias_far = jnp.where(remote_alive, 0.0, -jnp.inf).astype(f32)
    bias = jnp.concatenate([jnp.zeros((nblk, near_count), f32), bias_far], axis=1)
    bias = jnp.repeat(bias, bsize, axis=1).reshape(nblk, 1, (near_count + far_count) * bsize)

    o, acc, slot_grads = fused_attention(
        local_keys.reshape(-1), remote_keys.reshape(-1), qkv, d_group, pool, bias, score_scale
    )

    attn = lax.all_to_all(
        o.reshape(nhead, rows, hwide), "head", split_axis=0, concat_axis=0, tiled=True
    )
    mixed_out = (
        xf + jnp.einsum("hre,hef->rf", attn, w_out_heads, preferred_element_type=f32)
    ).astype(bf16)

    returned = lax.all_to_all(
        slot_grads.reshape(ndom, pair_slots * bsize, 2 * hwide),
        "dom",
        split_axis=0,
        concat_axis=0,
        tiled=True,
    ).reshape(slots, bsize, 2 * hwide)
    d_qkv = finish_grads(send_ids, acc, returned, hwide)
    d_rows = lax.all_to_all(
        d_qkv.reshape(nhead, rows, 3 * hwide), "head", split_axis=0, concat_axis=0, tiled=True
    )
    d_hidden = jnp.einsum("hrc,hdc->rd", d_rows, w_heads, preferred_element_type=f32)
    d_normed = d_hidden * norm_gain
    d_input = inv * (d_normed - normed * jnp.mean(d_normed * normed, axis=1, keepdims=True))
    grad_x = (grad_y.astype(f32) + d_input).astype(bf16)
    return (mixed_out, grad_x)


def solution(mesh):
    return jax.shard_map(
        local,
        mesh=mesh,
        in_specs=(
            P(("dom", "head"), None),
            P(),
            P(),
            P(),
            P(("dom", "head"), None),
            P("dom", None),
            P("dom", None),
            P("dom", None, None),
            P(None, "dom"),
        ),
        out_specs=(P(("dom", "head"), None), P(("dom", "head"), None)),
        check_vma=False,
    )
```

```python
import math

import jax
import jax.numpy as jnp
from jax import lax
from jax.experimental import pallas as pl
from jax.experimental.pallas import tpu as pltpu
from jax.sharding import PartitionSpec as P

HEADS = 8
EPS = 1e-05


def attention_kernel(
    lk_ref, rk_ref, qkv_ref, do_ref, pool_ref, bias_ref, o_ref, dq_ref, acc_ref, slot_ref, slot_acc,
    *, near, far, bsize, depth, scale
):
    f32 = jnp.float32
    bf16 = jnp.bfloat16
    nq = qkv_ref.shape[0]
    acc_ref[...] = jnp.zeros(acc_ref.shape, f32)
    slot_acc[...] = jnp.zeros(slot_acc.shape, f32)
    kcols = pl.ds(0, depth)
    vcols = pl.ds(depth, depth)
    qcols = pl.ds(2 * depth, depth)
    nt = (((1,), (1,)), ((), ()))

    def body(b, carry):
        q = qkv_ref[b, :, qcols]
        do = do_ref[b]
        ids_l = [lk_ref[b * near + i] for i in range(near)]
        ids_r = [rk_ref[b * far + i] for i in range(far)]
        keys = jnp.concatenate(
            [qkv_ref[i, :, kcols] for i in ids_l] + [pool_ref[i, :, kcols] for i in ids_r], axis=0
        )
        vals = jnp.concatenate(
            [qkv_ref[i, :, vcols] for i in ids_l] + [pool_ref[i, :, vcols] for i in ids_r], axis=0
        )
        q_s = q * scale
        do_s = do * scale
        s = lax.dot_general(q_s, keys, nt, preferred_element_type=f32)
        s = s + bias_ref[pl.ds(b, 1), :]
        top = jnp.max(s, axis=1, keepdims=True)
        expo = jnp.exp(s - top)
        total = jnp.sum(expo, axis=1, keepdims=True)
        w = (expo * (1.0 / total)).astype(bf16)
        o = jnp.dot(w, vals, preferred_element_type=f32).astype(bf16)
        o_ref[b] = o
        delta = jnp.sum(do_s.astype(f32) * o.astype(f32), axis=1, keepdims=True)
        dw = lax.dot_general(do_s, vals, nt, preferred_element_type=f32)
        ds = (w.astype(f32) * (dw - delta)).astype(bf16)
        dq_ref[b] = jnp.dot(ds, keys, preferred_element_type=f32)
        dk_t = jnp.dot(q.T, ds, preferred_element_type=f32)
        dv_t = jnp.dot(do.T, w, preferred_element_type=f32)
        dkv_t = jnp.concatenate([dk_t, dv_t], axis=0)
        for i in range(near):
            part = dkv_t[:, i * bsize:(i + 1) * bsize]
            acc_ref[ids_l[i]] = acc_ref[ids_l[i]] + part
        for i in range(far):
            part = dkv_t[:, (near + i) * bsize:(near + i + 1) * bsize]
            slot_acc[ids_r[i]] = slot_acc[ids_r[i]] + part
        return carry

    lax.fori_loop(0, nq, body, 0)
    slot_ref[...] = slot_acc[...].astype(bf16)


def fused_attention(local_ids, remote_ids, qkv, d_out, pool, bias, scale):
    nq, bsize, depth = d_out.shape
    near = local_ids.size // nq
    far = remote_ids.size // nq
    npool = pool.shape[0]
    f32 = jnp.float32
    smem = pl.BlockSpec(memory_space=pltpu.SMEM)
    vmem = pl.BlockSpec(memory_space=pltpu.VMEM)
    kernel = lambda *refs: attention_kernel(
        *refs, near=near, far=far, bsize=bsize, depth=depth, scale=scale
    )
    kv_t = (2 * depth, bsize)
    return pl.pallas_call(
        kernel,
        out_shape=(
            jax.ShapeDtypeStruct((nq, bsize, depth), jnp.bfloat16),
            jax.ShapeDtypeStruct((nq, bsize, depth), f32),
            jax.ShapeDtypeStruct((nq,) + kv_t, f32),
            jax.ShapeDtypeStruct((npool,) + kv_t, jnp.bfloat16),
        ),
        in_specs=[smem, smem] + [vmem] * 4,
        out_specs=(vmem, vmem, vmem, vmem),
        scratch_shapes=[pltpu.VMEM((npool,) + kv_t, f32)],
        compiler_params=pltpu.CompilerParams(vmem_limit_bytes=60 * 1024 * 1024),
    )(local_ids, remote_ids, qkv, d_out, pool, bias)


def finish_kernel(ids_ref, dq_ref, acc_ref, ret_ref, out_ref, total_ref):
    kvw = acc_ref.shape[1]
    qw = dq_ref.shape[2]
    total_ref[...] = acc_ref[...]

    def add_slot(j, carry):
        i = ids_ref[j]
        total_ref[i] = total_ref[i] + ret_ref[j].astype(jnp.float32)
        return carry

    lax.fori_loop(0, ret_ref.shape[0], add_slot, 0, unroll=8)

    def emit(b, carry):
        out_ref[b, :, pl.ds(0, kvw)] = total_ref[b].T.astype(jnp.bfloat16)
        out_ref[b, :, pl.ds(kvw, qw)] = dq_ref[b].astype(jnp.bfloat16)
        return carry

    lax.fori_loop(0, acc_ref.shape[0], emit, 0, unroll=4)


def finish_grads(send_ids, d_q, acc, returned):
    nq, bsize, depth = d_q.shape
    smem = pl.BlockSpec(memory_space=pltpu.SMEM)
    vmem = pl.BlockSpec(memory_space=pltpu.VMEM)
    return pl.pallas_call(
        finish_kernel,
        out_shape=jax.ShapeDtypeStruct((nq, bsize, acc.shape[1] + depth), jnp.bfloat16),
        in_specs=[smem, vmem, vmem, vmem],
        out_specs=vmem,
        scratch_shapes=[pltpu.VMEM(acc.shape, jnp.float32)],
        compiler_params=pltpu.CompilerParams(vmem_limit_bytes=60 * 1024 * 1024),
    )(send_ids, d_q, acc, returned)


def local(
    features,
    norm_gain,
    w_qkv,
    w_out,
    grad_y,
    local_keys,
    remote_keys,
    boundary_blocks,
    boundary_count,
):
    f32 = jnp.float32
    bf16 = jnp.bfloat16
    nhead = lax.axis_size("head")
    rows, width = features.shape
    per = HEADS // nhead
    depth = width // HEADS
    hwide = per * depth
    nblk, near_count = local_keys.shape
    far_count = remote_keys.shape[1]
    ndom = boundary_blocks.shape[1]
    pair_slots = boundary_blocks.shape[2]
    slots = ndom * pair_slots
    grows = rows * nhead
    bsize = grows // nblk
    score_scale = 1.0 / math.sqrt(depth)

    xf = features.astype(f32)
    inv = lax.rsqrt(jnp.mean(xf * xf, axis=1, keepdims=True) + EPS)
    normed = xf * inv
    hidden = (normed * norm_gain).astype(bf16)
    w_heads = (
        w_qkv.reshape(width, 3, nhead, hwide)[:, jnp.array([1, 2, 0])]
        .transpose(2, 0, 1, 3)
        .reshape(nhead, width, 3 * hwide)
    )
    w_out_heads = w_out.reshape(nhead, hwide, width)
    qkv_own = jnp.einsum("rd,hdc->hrc", hidden, w_heads, preferred_element_type=f32).astype(bf16)
    qkv = lax.all_to_all(qkv_own, "head", split_axis=0, concat_axis=0, tiled=True).reshape(
        nblk, bsize, 3 * hwide
    )

    d_attn = jnp.einsum("rf,hef->hre", grad_y, w_out_heads, preferred_element_type=f32).astype(bf16)
    d_group = lax.all_to_all(d_attn, "head", split_axis=0, concat_axis=0, tiled=True).reshape(
        nblk, bsize, hwide
    )

    send_ids = boundary_blocks[0].reshape(slots)
    outgoing = jnp.take(qkv[:, :, : 2 * hwide], send_ids, axis=0, mode="clip")
    pool = lax.all_to_all(
        outgoing.reshape(ndom, pair_slots * bsize, 2 * hwide),
        "dom",
        split_axis=0,
        concat_axis=0,
        tiled=True,
    ).reshape(slots, bsize, 2 * hwide)
    slot_alive = (jnp.arange(pair_slots, dtype=jnp.int32)[None, :] < boundary_count).reshape(slots)
    remote_alive = jnp.take(slot_alive, remote_keys, axis=0, mode="clip")
    bias_far = jnp.where(remote_alive, 0.0, -jnp.inf).astype(f32)
    bias = jnp.concatenate([jnp.zeros((nblk, near_count), f32), bias_far], axis=1)
    bias = jnp.repeat(bias, bsize, axis=1)

    o, d_q, acc, slot_grads = fused_attention(
        local_keys.reshape(-1), remote_keys.reshape(-1), qkv, d_group, pool, bias, score_scale
    )

    attn = lax.all_to_all(
        o.reshape(nhead, rows, hwide), "head", split_axis=0, concat_axis=0, tiled=True
    )
    mixed_out = (
        xf + jnp.einsum("hre,hef->rf", attn, w_out_heads, preferred_element_type=f32)
    ).astype(bf16)

    returned = lax.all_to_all(
        slot_grads.reshape(ndom, pair_slots * 2 * hwide, bsize),
        "dom",
        split_axis=0,
        concat_axis=0,
        tiled=True,
    ).reshape(slots, 2 * hwide, bsize)
    d_qkv = finish_grads(send_ids, d_q, acc, returned)
    d_rows = lax.all_to_all(
        d_qkv.reshape(nhead, rows, 3 * hwide), "head", split_axis=0, concat_axis=0, tiled=True
    )
    d_hidden = jnp.einsum("hrc,hdc->rd", d_rows, w_heads, preferred_element_type=f32)
    d_normed = d_hidden * norm_gain
    d_input = inv * (d_normed - normed * jnp.mean(d_normed * normed, axis=1, keepdims=True))
    grad_x = (grad_y.astype(f32) + d_input).astype(bf16)
    return (mixed_out, grad_x)


def solution(mesh):
    return jax.shard_map(
        local,
        mesh=mesh,
        in_specs=(
            P(("dom", "head"), None),
            P(),
            P(),
            P(),
            P(("dom", "head"), None),
            P("dom", None),
            P("dom", None),
            P("dom", None, None),
            P(None, "dom"),
        ),
        out_specs=(P(("dom", "head"), None), P(("dom", "head"), None)),
        check_vma=False,
    )
```

```python
import math

import jax
import jax.numpy as jnp
from jax import lax
from jax.experimental import pallas as pl
from jax.experimental.pallas import tpu as pltpu
from jax.sharding import PartitionSpec as P

HEADS = 8
EPS = 1e-05


def attention_kernel(
    lk_ref, rk_ref, q_ref, kv_ref, do_ref, pool_ref, bias_ref, o_ref, dq_ref, acc_ref, slot_ref, slot_acc,
    *, near, far, bsize, depth, scale
):
    f32 = jnp.float32
    bf16 = jnp.bfloat16
    nq = q_ref.shape[0]
    acc_ref[...] = jnp.zeros(acc_ref.shape, f32)
    slot_acc[...] = jnp.zeros(slot_acc.shape, f32)
    kcols = pl.ds(0, depth)
    vcols = pl.ds(depth, depth)
    nt = (((1,), (1,)), ((), ()))

    def body(b, carry):
        q = q_ref[b]
        do = do_ref[b]
        ids_l = [lk_ref[b * near + i] for i in range(near)]
        ids_r = [rk_ref[b * far + i] for i in range(far)]
        keys = jnp.concatenate(
            [kv_ref[i, :, kcols] for i in ids_l] + [pool_ref[i, :, kcols] for i in ids_r], axis=0
        )
        vals = jnp.concatenate(
            [kv_ref[i, :, vcols] for i in ids_l] + [pool_ref[i, :, vcols] for i in ids_r], axis=0
        )
        q_s = q * scale
        do_s = do * scale
        s = lax.dot_general(q_s, keys, nt, preferred_element_type=f32)
        s = s + bias_ref[pl.ds(b, 1), :]
        top = jnp.max(s, axis=1, keepdims=True)
        expo = jnp.exp(s - top)
        total = jnp.sum(expo, axis=1, keepdims=True)
        w = (expo * (1.0 / total)).astype(bf16)
        o = jnp.dot(w, vals, preferred_element_type=f32).astype(bf16)
        o_ref[b] = o
        delta = jnp.sum(do_s.astype(f32) * o.astype(f32), axis=1, keepdims=True)
        dw = lax.dot_general(do_s, vals, nt, preferred_element_type=f32)
        ds = (w.astype(f32) * (dw - delta)).astype(bf16)
        dq_ref[b] = jnp.dot(ds, keys, preferred_element_type=f32).astype(bf16)
        dk_t = jnp.dot(q.T, ds, preferred_element_type=f32)
        dv_t = jnp.dot(do.T, w, preferred_element_type=f32)
        dkv_t = jnp.concatenate([dk_t, dv_t], axis=0)
        for i in range(near):
            part = dkv_t[:, i * bsize:(i + 1) * bsize]
            acc_ref[ids_l[i]] = acc_ref[ids_l[i]] + part
        for i in range(far):
            part = dkv_t[:, (near + i) * bsize:(near + i + 1) * bsize]
            slot_acc[ids_r[i]] = slot_acc[ids_r[i]] + part
        return carry

    lax.fori_loop(0, nq, body, 0, unroll=2)
    slot_ref[...] = slot_acc[...].astype(bf16)


def fused_attention(local_ids, remote_ids, q, kv, d_out, pool, bias, scale):
    nq, bsize, depth = d_out.shape
    near = local_ids.size // nq
    far = remote_ids.size // nq
    npool = pool.shape[0]
    f32 = jnp.float32
    smem = pl.BlockSpec(memory_space=pltpu.SMEM)
    vmem = pl.BlockSpec(memory_space=pltpu.VMEM)
    kernel = lambda *refs: attention_kernel(
        *refs, near=near, far=far, bsize=bsize, depth=depth, scale=scale
    )
    kv_t = (2 * depth, bsize)
    return pl.pallas_call(
        kernel,
        out_shape=(
            jax.ShapeDtypeStruct((nq, bsize, depth), jnp.bfloat16),
            jax.ShapeDtypeStruct((nq, bsize, depth), jnp.bfloat16),
            jax.ShapeDtypeStruct((nq,) + kv_t, f32),
            jax.ShapeDtypeStruct((npool,) + kv_t, jnp.bfloat16),
        ),
        in_specs=[smem, smem] + [vmem] * 5,
        out_specs=(vmem, vmem, vmem, vmem),
        scratch_shapes=[pltpu.VMEM((npool,) + kv_t, f32)],
        compiler_params=pltpu.CompilerParams(vmem_limit_bytes=60 * 1024 * 1024),
    )(local_ids, remote_ids, q, kv, d_out, pool, bias)


def finish_kernel(ids_ref, acc_ref, ret_ref, out_ref, total_ref):
    total_ref[...] = acc_ref[...]

    def add_slot(j, carry):
        i = ids_ref[j]
        total_ref[i] = total_ref[i] + ret_ref[j].astype(jnp.float32)
        return carry

    lax.fori_loop(0, ret_ref.shape[0], add_slot, 0, unroll=8)

    def emit(b, carry):
        out_ref[b] = total_ref[b].T.astype(jnp.bfloat16)
        return carry

    lax.fori_loop(0, acc_ref.shape[0], emit, 0, unroll=4)


def finish_grads(send_ids, acc, returned):
    nq, kvw, bsize = acc.shape
    smem = pl.BlockSpec(memory_space=pltpu.SMEM)
    vmem = pl.BlockSpec(memory_space=pltpu.VMEM)
    return pl.pallas_call(
        finish_kernel,
        out_shape=jax.ShapeDtypeStruct((nq, bsize, kvw), jnp.bfloat16),
        in_specs=[smem, vmem, vmem],
        out_specs=vmem,
        scratch_shapes=[pltpu.VMEM(acc.shape, jnp.float32)],
        compiler_params=pltpu.CompilerParams(vmem_limit_bytes=60 * 1024 * 1024),
    )(send_ids, acc, returned)


def head_exchange(x, axis):
    n = x.shape[0]
    me = lax.axis_index(axis)
    twice = jnp.concatenate([x, x], axis=0)
    rot = lax.dynamic_slice_in_dim(twice, me, n, axis=0)
    recv = [rot[0]]
    for k in range(1, n):
        perm = [(i, (i + k) % n) for i in range(n)]
        recv.append(lax.ppermute(rot[k], axis, perm))
    back = jnp.stack([recv[0]] + recv[1:][::-1], axis=0)
    twice = jnp.concatenate([back, back], axis=0)
    return lax.dynamic_slice_in_dim(twice, (n - me) % n, n, axis=0)


def local(
    features,
    norm_gain,
    w_qkv,
    w_out,
    grad_y,
    local_keys,
    remote_keys,
    boundary_blocks,
    boundary_count,
):
    f32 = jnp.float32
    bf16 = jnp.bfloat16
    nhead = lax.axis_size("head")
    rows, width = features.shape
    per = HEADS // nhead
    depth = width // HEADS
    hwide = per * depth
    nblk, near_count = local_keys.shape
    far_count = remote_keys.shape[1]
    ndom = boundary_blocks.shape[1]
    pair_slots = boundary_blocks.shape[2]
    slots = ndom * pair_slots
    grows = rows * nhead
    bsize = grows // nblk
    score_scale = 1.0 / math.sqrt(depth)

    xf = features.astype(f32)
    inv = lax.rsqrt(jnp.mean(xf * xf, axis=1, keepdims=True) + EPS)
    normed = xf * inv
    hidden = (normed * norm_gain).astype(bf16)
    w_split = w_qkv.reshape(width, 3, nhead, hwide).transpose(2, 0, 1, 3)
    w_q = w_split[:, :, 0]
    w_kv = w_split[:, :, 1:].reshape(nhead, width, 2 * hwide)
    w_out_heads = w_out.reshape(nhead, hwide, width)
    kv_own = jnp.einsum("rd,hdc->hrc", hidden, w_kv, preferred_element_type=f32).astype(bf16)
    kv = lax.all_to_all(kv_own, "head", split_axis=0, concat_axis=0, tiled=True).reshape(
        nblk, bsize, 2 * hwide
    )
    q_own = jnp.einsum("rd,hdc->hrc", hidden, w_q, preferred_element_type=f32).astype(bf16)
    queries = head_exchange(q_own, "head").reshape(nblk, bsize, hwide)

    d_attn = jnp.einsum("rf,hef->hre", grad_y, w_out_heads, preferred_element_type=f32).astype(bf16)
    d_group = head_exchange(d_attn, "head").reshape(nblk, bsize, hwide)

    send_ids = boundary_blocks[0].reshape(slots)
    outgoing = jnp.take(kv, send_ids, axis=0, mode="clip")
    pool = lax.all_to_all(
        outgoing.reshape(ndom, pair_slots * bsize, 2 * hwide),
        "dom",
        split_axis=0,
        concat_axis=0,
        tiled=True,
    ).reshape(slots, bsize, 2 * hwide)
    slot_alive = (jnp.arange(pair_slots, dtype=jnp.int32)[None, :] < boundary_count).reshape(slots)
    remote_alive = jnp.take(slot_alive, remote_keys, axis=0, mode="clip")
    bias_far = jnp.where(remote_alive, 0.0, -jnp.inf).astype(f32)
    bias = jnp.concatenate([jnp.zeros((nblk, near_count), f32), bias_far], axis=1)
    bias = jnp.repeat(bias, bsize, axis=1)

    o, d_q, acc, slot_grads = fused_attention(
        local_keys.reshape(-1), remote_keys.reshape(-1), queries, kv, d_group, pool, bias,
        score_scale,
    )

    attn = head_exchange(o.reshape(nhead, rows, hwide), "head")
    mixed_out = (
        xf + jnp.einsum("hre,hef->rf", attn, w_out_heads, preferred_element_type=f32)
    ).astype(bf16)
    d_rows_q = head_exchange(d_q.reshape(nhead, rows, hwide), "head")
    d_hidden_q = jnp.einsum("hrc,hdc->rd", d_rows_q, w_q, preferred_element_type=f32)

    returned = lax.all_to_all(
        slot_grads.reshape(ndom, pair_slots * 2 * hwide, bsize),
        "dom",
        split_axis=0,
        concat_axis=0,
        tiled=True,
    ).reshape(slots, 2 * hwide, bsize)
    d_kv = finish_grads(send_ids, acc, returned)
    d_rows = lax.all_to_all(
        d_kv.reshape(nhead, rows, 2 * hwide), "head", split_axis=0, concat_axis=0, tiled=True
    )
    d_hidden = d_hidden_q + jnp.einsum("hrc,hdc->rd", d_rows, w_kv, preferred_element_type=f32)
    d_normed = d_hidden * norm_gain
    d_input = inv * (d_normed - normed * jnp.mean(d_normed * normed, axis=1, keepdims=True))
    grad_x = (grad_y.astype(f32) + d_input).astype(bf16)
    return (mixed_out, grad_x)


def solution(mesh):
    return jax.shard_map(
        local,
        mesh=mesh,
        in_specs=(
            P(("dom", "head"), None),
            P(),
            P(),
            P(),
            P(("dom", "head"), None),
            P("dom", None),
            P("dom", None),
            P("dom", None, None),
            P(None, "dom"),
        ),
        out_specs=(P(("dom", "head"), None), P(("dom", "head"), None)),
        check_vma=False,
    )
```

```python
import math

import jax
import jax.numpy as jnp
from jax import lax
from jax.experimental import pallas as pl
from jax.experimental.pallas import tpu as pltpu
from jax.sharding import PartitionSpec as P

HEADS = 8
EPS = 1e-05


def attention_kernel(
    lk_ref, rk_ref, q_ref, kv_ref, do_ref, pool_ref, bias_ref, o_ref, dq_ref, acc_ref, slot_ref, slot_acc,
    *, near, far, bsize, depth, scale
):
    f32 = jnp.float32
    bf16 = jnp.bfloat16
    nq = q_ref.shape[0]
    acc_ref[...] = jnp.zeros(acc_ref.shape, f32)
    slot_acc[...] = jnp.zeros(slot_acc.shape, f32)
    kcols = pl.ds(0, depth)
    vcols = pl.ds(depth, depth)
    nt = (((1,), (1,)), ((), ()))

    def body(b, carry):
        q = q_ref[b]
        do = do_ref[b]
        ids_l = [lk_ref[b * near + i] for i in range(near)]
        ids_r = [rk_ref[b * far + i] for i in range(far)]
        keys = jnp.concatenate(
            [kv_ref[i, :, kcols] for i in ids_l] + [pool_ref[i, :, kcols] for i in ids_r], axis=0
        )
        vals = jnp.concatenate(
            [kv_ref[i, :, vcols] for i in ids_l] + [pool_ref[i, :, vcols] for i in ids_r], axis=0
        )
        q_s = q * scale
        do_s = do * scale
        s = lax.dot_general(q_s, keys, nt, preferred_element_type=f32)
        s = s + bias_ref[pl.ds(b, 1), :]
        top = jnp.max(s, axis=1, keepdims=True)
        expo = jnp.exp(s - top)
        total = jnp.sum(expo, axis=1, keepdims=True)
        w = (expo * (1.0 / total)).astype(bf16)
        o = jnp.dot(w, vals, preferred_element_type=f32).astype(bf16)
        o_ref[b] = o
        delta = jnp.sum(do_s.astype(f32) * o.astype(f32), axis=1, keepdims=True)
        dw = lax.dot_general(do_s, vals, nt, preferred_element_type=f32)
        ds = (w.astype(f32) * (dw - delta)).astype(bf16)
        dq_ref[b] = jnp.dot(ds, keys, preferred_element_type=f32).astype(bf16)
        dk_t = jnp.dot(q.T, ds, preferred_element_type=f32)
        dv_t = jnp.dot(do.T, w, preferred_element_type=f32)
        dkv_t = jnp.concatenate([dk_t, dv_t], axis=0)
        for i in range(near):
            part = dkv_t[:, i * bsize:(i + 1) * bsize]
            acc_ref[ids_l[i]] = acc_ref[ids_l[i]] + part
        for i in range(far):
            part = dkv_t[:, (near + i) * bsize:(near + i + 1) * bsize]
            slot_acc[ids_r[i]] = slot_acc[ids_r[i]] + part
        return carry

    lax.fori_loop(0, nq, body, 0, unroll=2)
    slot_ref[...] = slot_acc[...].astype(bf16)


def fused_attention(local_ids, remote_ids, q, kv, d_out, pool, bias, scale):
    nq, bsize, depth = d_out.shape
    near = local_ids.size // nq
    far = remote_ids.size // nq
    npool = pool.shape[0]
    f32 = jnp.float32
    smem = pl.BlockSpec(memory_space=pltpu.SMEM)
    vmem = pl.BlockSpec(memory_space=pltpu.VMEM)
    kernel = lambda *refs: attention_kernel(
        *refs, near=near, far=far, bsize=bsize, depth=depth, scale=scale
    )
    kv_t = (2 * depth, bsize)
    return pl.pallas_call(
        kernel,
        out_shape=(
            jax.ShapeDtypeStruct((nq, bsize, depth), jnp.bfloat16),
            jax.ShapeDtypeStruct((nq, bsize, depth), jnp.bfloat16),
            jax.ShapeDtypeStruct((nq,) + kv_t, f32),
            jax.ShapeDtypeStruct((npool,) + kv_t, jnp.bfloat16),
        ),
        in_specs=[smem, smem] + [vmem] * 5,
        out_specs=(vmem, vmem, vmem, vmem),
        scratch_shapes=[pltpu.VMEM((npool,) + kv_t, f32)],
        compiler_params=pltpu.CompilerParams(vmem_limit_bytes=60 * 1024 * 1024),
    )(local_ids, remote_ids, q, kv, d_out, pool, bias)


def finish_kernel(ids_ref, acc_ref, ret_ref, out_ref, total_ref):
    total_ref[...] = acc_ref[...]

    def add_slot(j, carry):
        i = ids_ref[j]
        total_ref[i] = total_ref[i] + ret_ref[j].astype(jnp.float32)
        return carry

    lax.fori_loop(0, ret_ref.shape[0], add_slot, 0, unroll=8)

    def emit(b, carry):
        out_ref[b] = total_ref[b].T.astype(jnp.bfloat16)
        return carry

    lax.fori_loop(0, acc_ref.shape[0], emit, 0, unroll=4)


def finish_grads(send_ids, acc, returned):
    nq, kvw, bsize = acc.shape
    smem = pl.BlockSpec(memory_space=pltpu.SMEM)
    vmem = pl.BlockSpec(memory_space=pltpu.VMEM)
    return pl.pallas_call(
        finish_kernel,
        out_shape=jax.ShapeDtypeStruct((nq, bsize, kvw), jnp.bfloat16),
        in_specs=[smem, vmem, vmem],
        out_specs=vmem,
        scratch_shapes=[pltpu.VMEM(acc.shape, jnp.float32)],
        compiler_params=pltpu.CompilerParams(vmem_limit_bytes=60 * 1024 * 1024),
    )(send_ids, acc, returned)


def head_exchange(x, axis):
    n = x.shape[0]
    me = lax.axis_index(axis)
    twice = jnp.concatenate([x, x], axis=0)
    rot = lax.dynamic_slice_in_dim(twice, me, n, axis=0)
    recv = [rot[0]]
    for k in range(1, n):
        perm = [(i, (i + k) % n) for i in range(n)]
        recv.append(lax.ppermute(rot[k], axis, perm))
    back = jnp.stack([recv[0]] + recv[1:][::-1], axis=0)
    twice = jnp.concatenate([back, back], axis=0)
    return lax.dynamic_slice_in_dim(twice, (n - me) % n, n, axis=0)


def local(
    features,
    norm_gain,
    w_qkv,
    w_out,
    grad_y,
    local_keys,
    remote_keys,
    boundary_blocks,
    boundary_count,
):
    f32 = jnp.float32
    bf16 = jnp.bfloat16
    nhead = lax.axis_size("head")
    rows, width = features.shape
    per = HEADS // nhead
    depth = width // HEADS
    hwide = per * depth
    nblk, near_count = local_keys.shape
    far_count = remote_keys.shape[1]
    ndom = boundary_blocks.shape[1]
    pair_slots = boundary_blocks.shape[2]
    slots = ndom * pair_slots
    grows = rows * nhead
    bsize = grows // nblk
    score_scale = 1.0 / math.sqrt(depth)

    xf = features.astype(f32)
    inv = lax.rsqrt(jnp.mean(xf * xf, axis=1, keepdims=True) + EPS)
    normed = xf * inv
    hidden = (normed * norm_gain).astype(bf16)
    w_split = w_qkv.reshape(width, 3, nhead, hwide).transpose(2, 0, 1, 3)
    w_q = w_split[:, :, 0]
    w_kv = w_split[:, :, 1:].reshape(nhead, width, 2 * hwide)
    w_out_heads = w_out.reshape(nhead, hwide, width)
    kv_own = jnp.einsum("rd,hdc->hrc", hidden, w_kv, preferred_element_type=f32).astype(bf16)
    kv = lax.all_to_all(kv_own, "head", split_axis=0, concat_axis=0, tiled=True).reshape(
        nblk, bsize, 2 * hwide
    )
    q_own = jnp.einsum("rd,hdc->hrc", hidden, w_q, preferred_element_type=f32).astype(bf16)
    d_attn = jnp.einsum("rf,hef->hre", grad_y, w_out_heads, preferred_element_type=f32).astype(bf16)

    send_ids = boundary_blocks[0].reshape(slots)
    outgoing = jnp.take(kv, send_ids, axis=0, mode="clip")
    outgoing, q_own, d_attn = lax.optimization_barrier((outgoing, q_own, d_attn))
    queries = head_exchange(q_own, "head").reshape(nblk, bsize, hwide)
    d_group = head_exchange(d_attn, "head").reshape(nblk, bsize, hwide)
    pool = lax.all_to_all(
        outgoing.reshape(ndom, pair_slots * bsize, 2 * hwide),
        "dom",
        split_axis=0,
        concat_axis=0,
        tiled=True,
    ).reshape(slots, bsize, 2 * hwide)
    slot_alive = (jnp.arange(pair_slots, dtype=jnp.int32)[None, :] < boundary_count).reshape(slots)
    remote_alive = jnp.take(slot_alive, remote_keys, axis=0, mode="clip")
    bias_far = jnp.where(remote_alive, 0.0, -jnp.inf).astype(f32)
    bias = jnp.concatenate([jnp.zeros((nblk, near_count), f32), bias_far], axis=1)
    bias = jnp.repeat(bias, bsize, axis=1)

    o, d_q, acc, slot_grads = fused_attention(
        local_keys.reshape(-1), remote_keys.reshape(-1), queries, kv, d_group, pool, bias,
        score_scale,
    )

    attn = head_exchange(o.reshape(nhead, rows, hwide), "head")
    mixed_out = (
        xf + jnp.einsum("hre,hef->rf", attn, w_out_heads, preferred_element_type=f32)
    ).astype(bf16)
    d_rows_q = head_exchange(d_q.reshape(nhead, rows, hwide), "head")
    d_hidden_q = jnp.einsum("hrc,hdc->rd", d_rows_q, w_q, preferred_element_type=f32)

    returned = lax.all_to_all(
        slot_grads.reshape(ndom, pair_slots * 2 * hwide, bsize),
        "dom",
        split_axis=0,
        concat_axis=0,
        tiled=True,
    ).reshape(slots, 2 * hwide, bsize)
    d_kv = finish_grads(send_ids, acc, returned)
    d_rows = lax.all_to_all(
        d_kv.reshape(nhead, rows, 2 * hwide), "head", split_axis=0, concat_axis=0, tiled=True
    )
    d_hidden = d_hidden_q + jnp.einsum("hrc,hdc->rd", d_rows, w_kv, preferred_element_type=f32)
    d_normed = d_hidden * norm_gain
    d_input = inv * (d_normed - normed * jnp.mean(d_normed * normed, axis=1, keepdims=True))
    grad_x = (grad_y.astype(f32) + d_input).astype(bf16)
    return (mixed_out, grad_x)


def solution(mesh):
    return jax.shard_map(
        local,
        mesh=mesh,
        in_specs=(
            P(("dom", "head"), None),
            P(),
            P(),
            P(),
            P(("dom", "head"), None),
            P("dom", None),
            P("dom", None),
            P("dom", None, None),
            P(None, "dom"),
        ),
        out_specs=(P(("dom", "head"), None), P(("dom", "head"), None)),
        check_vma=False,
    )
```

```python
import math

import jax
import jax.numpy as jnp
from jax import lax
from jax.experimental import pallas as pl
from jax.experimental.pallas import tpu as pltpu
from jax.sharding import PartitionSpec as P

HEADS = 8
EPS = 1e-05


def attention_kernel(
    lk_ref, rk_ref, q_ref, kv_ref, do_ref, pool_ref, bias_ref, o_ref, dq_ref, acc_ref, slot_ref, slot_acc,
    *, near, far, bsize, depth, scale
):
    f32 = jnp.float32
    bf16 = jnp.bfloat16
    nq = q_ref.shape[0]
    acc_ref[...] = jnp.zeros(acc_ref.shape, f32)
    slot_acc[...] = jnp.zeros(slot_acc.shape, f32)
    kcols = pl.ds(0, depth)
    vcols = pl.ds(depth, depth)
    nt = (((1,), (1,)), ((), ()))

    def body(b, carry):
        q = q_ref[b]
        do = do_ref[b]
        ids_l = [lk_ref[b * near + i] for i in range(near)]
        ids_r = [rk_ref[b * far + i] for i in range(far)]
        keys = jnp.concatenate(
            [kv_ref[i, :, kcols] for i in ids_l] + [pool_ref[i, :, kcols] for i in ids_r], axis=0
        )
        vals = jnp.concatenate(
            [kv_ref[i, :, vcols] for i in ids_l] + [pool_ref[i, :, vcols] for i in ids_r], axis=0
        )
        q_s = q * scale
        do_s = do * scale
        s = lax.dot_general(q_s, keys, nt, preferred_element_type=f32)
        s = s + bias_ref[pl.ds(b, 1), :]
        top = jnp.max(s, axis=1, keepdims=True)
        expo = jnp.exp(s - top)
        total = jnp.sum(expo, axis=1, keepdims=True)
        w = (expo * (1.0 / total)).astype(bf16)
        o = jnp.dot(w, vals, preferred_element_type=f32).astype(bf16)
        o_ref[b] = o
        delta = jnp.sum(do_s.astype(f32) * o.astype(f32), axis=1, keepdims=True)
        dw = lax.dot_general(do_s, vals, nt, preferred_element_type=f32)
        ds = (w.astype(f32) * (dw - delta)).astype(bf16)
        dq_ref[b] = jnp.dot(ds, keys, preferred_element_type=f32).astype(bf16)
        dk_t = jnp.dot(q.T, ds, preferred_element_type=f32)
        dv_t = jnp.dot(do.T, w, preferred_element_type=f32)
        dkv_t = jnp.concatenate([dk_t, dv_t], axis=0)
        for i in range(near):
            part = dkv_t[:, i * bsize:(i + 1) * bsize]
            acc_ref[ids_l[i]] = acc_ref[ids_l[i]] + part
        for i in range(far):
            part = dkv_t[:, (near + i) * bsize:(near + i + 1) * bsize]
            slot_acc[ids_r[i]] = slot_acc[ids_r[i]] + part
        return carry

    lax.fori_loop(0, nq, body, 0, unroll=4)
    slot_ref[...] = slot_acc[...].astype(bf16)


def fused_attention(local_ids, remote_ids, q, kv, d_out, pool, bias, scale):
    nq, bsize, depth = d_out.shape
    near = local_ids.size // nq
    far = remote_ids.size // nq
    npool = pool.shape[0]
    f32 = jnp.float32
    smem = pl.BlockSpec(memory_space=pltpu.SMEM)
    vmem = pl.BlockSpec(memory_space=pltpu.VMEM)
    kernel = lambda *refs: attention_kernel(
        *refs, near=near, far=far, bsize=bsize, depth=depth, scale=scale
    )
    kv_t = (2 * depth, bsize)
    return pl.pallas_call(
        kernel,
        out_shape=(
            jax.ShapeDtypeStruct((nq, bsize, depth), jnp.bfloat16),
            jax.ShapeDtypeStruct((nq, bsize, depth), jnp.bfloat16),
            jax.ShapeDtypeStruct((nq,) + kv_t, f32),
            jax.ShapeDtypeStruct((npool,) + kv_t, jnp.bfloat16),
        ),
        in_specs=[smem, smem] + [vmem] * 5,
        out_specs=(vmem, vmem, vmem, vmem),
        scratch_shapes=[pltpu.VMEM((npool,) + kv_t, f32)],
        compiler_params=pltpu.CompilerParams(vmem_limit_bytes=60 * 1024 * 1024),
    )(local_ids, remote_ids, q, kv, d_out, pool, bias)


def finish_kernel(ids_ref, acc_ref, ret_ref, out_ref, total_ref):
    total_ref[...] = acc_ref[...]

    def add_slot(j, carry):
        i = ids_ref[j]
        total_ref[i] = total_ref[i] + ret_ref[j].astype(jnp.float32)
        return carry

    lax.fori_loop(0, ret_ref.shape[0], add_slot, 0, unroll=8)

    def emit(b, carry):
        out_ref[b] = total_ref[b].T.astype(jnp.bfloat16)
        return carry

    lax.fori_loop(0, acc_ref.shape[0], emit, 0, unroll=4)


def finish_grads(send_ids, acc, returned):
    nq, kvw, bsize = acc.shape
    smem = pl.BlockSpec(memory_space=pltpu.SMEM)
    vmem = pl.BlockSpec(memory_space=pltpu.VMEM)
    return pl.pallas_call(
        finish_kernel,
        out_shape=jax.ShapeDtypeStruct((nq, bsize, kvw), jnp.bfloat16),
        in_specs=[smem, vmem, vmem],
        out_specs=vmem,
        scratch_shapes=[pltpu.VMEM(acc.shape, jnp.float32)],
        compiler_params=pltpu.CompilerParams(vmem_limit_bytes=60 * 1024 * 1024),
    )(send_ids, acc, returned)


def head_exchange(x, axis):
    n = x.shape[0]
    me = lax.axis_index(axis)
    out = x
    for k in range(1, n):
        perm = [(i, (i + k) % n) for i in range(n)]
        part = lax.dynamic_index_in_dim(x, (me + k) % n, 0, keepdims=True)
        got = lax.ppermute(part, axis, perm)
        out = lax.dynamic_update_index_in_dim(out, got, (me + n - k) % n, 0)
    return out


def local(
    features,
    norm_gain,
    w_qkv,
    w_out,
    grad_y,
    local_keys,
    remote_keys,
    boundary_blocks,
    boundary_count,
):
    f32 = jnp.float32
    bf16 = jnp.bfloat16
    nhead = lax.axis_size("head")
    rows, width = features.shape
    per = HEADS // nhead
    depth = width // HEADS
    hwide = per * depth
    nblk, near_count = local_keys.shape
    far_count = remote_keys.shape[1]
    ndom = boundary_blocks.shape[1]
    pair_slots = boundary_blocks.shape[2]
    slots = ndom * pair_slots
    grows = rows * nhead
    bsize = grows // nblk
    score_scale = 1.0 / math.sqrt(depth)

    xf = features.astype(f32)
    inv = lax.rsqrt(jnp.mean(xf * xf, axis=1, keepdims=True) + EPS)
    normed = xf * inv
    hidden = (normed * norm_gain).astype(bf16)
    w_split = w_qkv.reshape(width, 3, nhead, hwide).transpose(2, 0, 1, 3)
    w_q = w_split[:, :, 0]
    w_kv = w_split[:, :, 1:].reshape(nhead, width, 2 * hwide)
    w_out_heads = w_out.reshape(nhead, hwide, width)
    kv_own = jnp.einsum("rd,hdc->hrc", hidden, w_kv, preferred_element_type=f32).astype(bf16)
    kv = lax.all_to_all(kv_own, "head", split_axis=0, concat_axis=0, tiled=True).reshape(
        nblk, bsize, 2 * hwide
    )
    q_own = jnp.einsum("rd,hdc->hrc", hidden, w_q, preferred_element_type=f32).astype(bf16)
    d_attn = jnp.einsum("rf,hef->hre", grad_y, w_out_heads, preferred_element_type=f32).astype(bf16)

    send_ids = boundary_blocks[0].reshape(slots)
    outgoing = jnp.take(kv, send_ids, axis=0, mode="clip")
    outgoing, q_own, d_attn = lax.optimization_barrier((outgoing, q_own, d_attn))
    queries = head_exchange(q_own, "head").reshape(nblk, bsize, hwide)
    d_group = head_exchange(d_attn, "head").reshape(nblk, bsize, hwide)
    pool = lax.all_to_all(
        outgoing.reshape(ndom, pair_slots * bsize, 2 * hwide),
        "dom",
        split_axis=0,
        concat_axis=0,
        tiled=True,
    ).reshape(slots, bsize, 2 * hwide)
    slot_alive = (jnp.arange(pair_slots, dtype=jnp.int32)[None, :] < boundary_count).reshape(slots)
    remote_alive = jnp.take(slot_alive, remote_keys, axis=0, mode="clip")
    bias_far = jnp.where(remote_alive, 0.0, -jnp.inf).astype(f32)
    bias = jnp.concatenate([jnp.zeros((nblk, near_count), f32), bias_far], axis=1)
    bias = jnp.repeat(bias, bsize, axis=1)

    o, d_q, acc, slot_grads = fused_attention(
        local_keys.reshape(-1), remote_keys.reshape(-1), queries, kv, d_group, pool, bias,
        score_scale,
    )

    attn = head_exchange(o.reshape(nhead, rows, hwide), "head")
    mixed_out = (
        xf + jnp.einsum("hre,hef->rf", attn, w_out_heads, preferred_element_type=f32)
    ).astype(bf16)
    d_rows_q = head_exchange(d_q.reshape(nhead, rows, hwide), "head")
    d_hidden_q = jnp.einsum("hrc,hdc->rd", d_rows_q, w_q, preferred_element_type=f32)

    returned = lax.all_to_all(
        slot_grads.reshape(ndom, pair_slots * 2 * hwide, bsize),
        "dom",
        split_axis=0,
        concat_axis=0,
        tiled=True,
    ).reshape(slots, 2 * hwide, bsize)
    d_kv = finish_grads(send_ids, acc, returned)
    d_rows = lax.all_to_all(
        d_kv.reshape(nhead, rows, 2 * hwide), "head", split_axis=0, concat_axis=0, tiled=True
    )
    d_hidden = d_hidden_q + jnp.einsum("hrc,hdc->rd", d_rows, w_kv, preferred_element_type=f32)
    d_normed = d_hidden * norm_gain
    d_input = inv * (d_normed - normed * jnp.mean(d_normed * normed, axis=1, keepdims=True))
    grad_x = (grad_y.astype(f32) + d_input).astype(bf16)
    return (mixed_out, grad_x)


def solution(mesh):
    return jax.shard_map(
        local,
        mesh=mesh,
        in_specs=(
            P(("dom", "head"), None),
            P(),
            P(),
            P(),
            P(("dom", "head"), None),
            P("dom", None),
            P("dom", None),
            P("dom", None, None),
            P(None, "dom"),
        ),
        out_specs=(P(("dom", "head"), None), P(("dom", "head"), None)),
        check_vma=False,
    )
```

```python
import math

import jax
import jax.numpy as jnp
from jax import lax
from jax.experimental import pallas as pl
from jax.experimental.pallas import tpu as pltpu
from jax.sharding import PartitionSpec as P

HEADS = 8
EPS = 1e-05


def load_blocks(kv_ref, pool_ref, ids_l, ids_r, cols):
    return jnp.concatenate(
        [kv_ref[i, :, cols] for i in ids_l] + [pool_ref[i, :, cols] for i in ids_r], axis=0
    )


def column_to_row(col):
    n = col.shape[0]
    return jnp.broadcast_to(col, (n, n)).T[0:1, :]


def row_to_column(row):
    n = row.shape[1]
    return jnp.broadcast_to(row, (n, n)).T[:, 0:1]


def remote_kernel(
    lk_ref, rk_ref, q_ref, kv_ref, do_ref, pool_ref, bias_ref, o_ref, dq_ref, stats_ref,
    slot_ref, slot_acc, *, near, far, bsize, depth, scale
):
    f32 = jnp.float32
    bf16 = jnp.bfloat16
    nq = q_ref.shape[0]
    slot_acc[...] = jnp.zeros(slot_acc.shape, f32)
    kcols = pl.ds(0, depth)
    vcols = pl.ds(depth, depth)
    nt = (((1,), (1,)), ((), ()))
    split = near * bsize

    def body(b, carry):
        q = q_ref[b]
        do = do_ref[b]
        ids_l = [lk_ref[b * near + i] for i in range(near)]
        ids_r = [rk_ref[b * far + i] for i in range(far)]
        keys = load_blocks(kv_ref, pool_ref, ids_l, ids_r, kcols)
        vals = load_blocks(kv_ref, pool_ref, ids_l, ids_r, vcols)
        q_s = q * scale
        do_s = do * scale
        s = lax.dot_general(q_s, keys, nt, preferred_element_type=f32)
        s = s + bias_ref[pl.ds(b, 1), :]
        top = jnp.max(s, axis=1, keepdims=True)
        expo = jnp.exp(s - top)
        total = jnp.sum(expo, axis=1, keepdims=True)
        rtot = 1.0 / total
        w = (expo * rtot).astype(bf16)
        o = jnp.dot(w, vals, preferred_element_type=f32).astype(bf16)
        o_ref[b] = o
        delta = jnp.sum(do_s.astype(f32) * o.astype(f32), axis=1, keepdims=True)
        stats_ref[b] = jnp.concatenate(
            [column_to_row(top), column_to_row(rtot), column_to_row(delta)], axis=0
        )
        keys_r = keys[split:]
        vals_r = vals[split:]
        w_r = w[:, split:]
        dw = lax.dot_general(do_s, vals_r, nt, preferred_element_type=f32)
        ds = (w_r.astype(f32) * (dw - delta)).astype(bf16)
        dq_ref[b] = jnp.dot(ds, keys_r, preferred_element_type=f32)
        dk_t = jnp.dot(q.T, ds, preferred_element_type=f32)
        dv_t = jnp.dot(do.T, w_r, preferred_element_type=f32)
        dkv_t = jnp.concatenate([dk_t, dv_t], axis=0)
        for i in range(far):
            part = dkv_t[:, i * bsize:(i + 1) * bsize]
            slot_acc[ids_r[i]] = slot_acc[ids_r[i]] + part
        return carry

    lax.fori_loop(0, nq, body, 0, unroll=4)
    slot_ref[...] = slot_acc[...].astype(bf16)


def local_kernel(
    lk_ref, q_ref, kv_ref, do_ref, stats_ref, dqr_ref, dq_ref, acc_ref,
    *, near, bsize, depth, scale
):
    f32 = jnp.float32
    bf16 = jnp.bfloat16
    nq = q_ref.shape[0]
    acc_ref[...] = jnp.zeros(acc_ref.shape, f32)
    kcols = pl.ds(0, depth)
    vcols = pl.ds(depth, depth)
    nt = (((1,), (1,)), ((), ()))

    def body(b, carry):
        q = q_ref[b]
        do = do_ref[b]
        ids_l = [lk_ref[b * near + i] for i in range(near)]
        keys = jnp.concatenate([kv_ref[i, :, kcols] for i in ids_l], axis=0)
        vals = jnp.concatenate([kv_ref[i, :, vcols] for i in ids_l], axis=0)
        q_s = q * scale
        do_s = do * scale
        stats = stats_ref[b]
        top = row_to_column(stats[0:1, :])
        rtot = row_to_column(stats[1:2, :])
        delta = row_to_column(stats[2:3, :])
        s = lax.dot_general(q_s, keys, nt, preferred_element_type=f32)
        w = (jnp.exp(s - top) * rtot).astype(bf16)
        dw = lax.dot_general(do_s, vals, nt, preferred_element_type=f32)
        ds = (w.astype(f32) * (dw - delta)).astype(bf16)
        dq = dqr_ref[b] + jnp.dot(ds, keys, preferred_element_type=f32)
        dq_ref[b] = dq.astype(bf16)
        dk_t = jnp.dot(q.T, ds, preferred_element_type=f32)
        dv_t = jnp.dot(do.T, w, preferred_element_type=f32)
        dkv_t = jnp.concatenate([dk_t, dv_t], axis=0)
        for i in range(near):
            part = dkv_t[:, i * bsize:(i + 1) * bsize]
            acc_ref[ids_l[i]] = acc_ref[ids_l[i]] + part
        return carry

    lax.fori_loop(0, nq, body, 0, unroll=4)


def fused_attention(local_ids, remote_ids, q, kv, d_out, pool, bias, scale):
    nq, bsize, depth = d_out.shape
    near = local_ids.size // nq
    far = remote_ids.size // nq
    npool = pool.shape[0]
    f32 = jnp.float32
    smem = pl.BlockSpec(memory_space=pltpu.SMEM)
    vmem = pl.BlockSpec(memory_space=pltpu.VMEM)
    kv_t = (2 * depth, bsize)
    params = pltpu.CompilerParams(vmem_limit_bytes=60 * 1024 * 1024)
    o, dq_r, stats, slot = pl.pallas_call(
        lambda *refs: remote_kernel(
            *refs, near=near, far=far, bsize=bsize, depth=depth, scale=scale
        ),
        out_shape=(
            jax.ShapeDtypeStruct((nq, bsize, depth), jnp.bfloat16),
            jax.ShapeDtypeStruct((nq, bsize, depth), f32),
            jax.ShapeDtypeStruct((nq, 3, bsize), f32),
            jax.ShapeDtypeStruct((npool,) + kv_t, jnp.bfloat16),
        ),
        in_specs=[smem, smem] + [vmem] * 5,
        out_specs=(vmem, vmem, vmem, vmem),
        scratch_shapes=[pltpu.VMEM((npool,) + kv_t, f32)],
        compiler_params=params,
    )(local_ids, remote_ids, q, kv, d_out, pool, bias)
    dq, acc = pl.pallas_call(
        lambda *refs: local_kernel(*refs, near=near, bsize=bsize, depth=depth, scale=scale),
        out_shape=(
            jax.ShapeDtypeStruct((nq, bsize, depth), jnp.bfloat16),
            jax.ShapeDtypeStruct((nq,) + kv_t, f32),
        ),
        in_specs=[smem] + [vmem] * 5,
        out_specs=(vmem, vmem),
        compiler_params=params,
    )(local_ids, q, kv, d_out, stats, dq_r)
    return o, dq, acc, slot


def finish_kernel(ids_ref, acc_ref, ret_ref, out_ref, total_ref):
    total_ref[...] = acc_ref[...]

    def add_slot(j, carry):
        i = ids_ref[j]
        total_ref[i] = total_ref[i] + ret_ref[j].astype(jnp.float32)
        return carry

    lax.fori_loop(0, ret_ref.shape[0], add_slot, 0, unroll=8)

    def emit(b, carry):
        out_ref[b] = total_ref[b].T.astype(jnp.bfloat16)
        return carry

    lax.fori_loop(0, acc_ref.shape[0], emit, 0, unroll=4)


def finish_grads(send_ids, acc, returned):
    nq, kvw, bsize = acc.shape
    smem = pl.BlockSpec(memory_space=pltpu.SMEM)
    vmem = pl.BlockSpec(memory_space=pltpu.VMEM)
    return pl.pallas_call(
        finish_kernel,
        out_shape=jax.ShapeDtypeStruct((nq, bsize, kvw), jnp.bfloat16),
        in_specs=[smem, vmem, vmem],
        out_specs=vmem,
        scratch_shapes=[pltpu.VMEM(acc.shape, jnp.float32)],
        compiler_params=pltpu.CompilerParams(vmem_limit_bytes=60 * 1024 * 1024),
    )(send_ids, acc, returned)


def head_exchange(x, axis):
    n = x.shape[0]
    me = lax.axis_index(axis)
    out = x
    for k in range(1, n):
        perm = [(i, (i + k) % n) for i in range(n)]
        part = lax.dynamic_index_in_dim(x, (me + k) % n, 0, keepdims=True)
        got = lax.ppermute(part, axis, perm)
        out = lax.dynamic_update_index_in_dim(out, got, (me + n - k) % n, 0)
    return out


def local(
    features,
    norm_gain,
    w_qkv,
    w_out,
    grad_y,
    local_keys,
    remote_keys,
    boundary_blocks,
    boundary_count,
):
    f32 = jnp.float32
    bf16 = jnp.bfloat16
    nhead = lax.axis_size("head")
    rows, width = features.shape
    per = HEADS // nhead
    depth = width // HEADS
    hwide = per * depth
    nblk, near_count = local_keys.shape
    far_count = remote_keys.shape[1]
    ndom = boundary_blocks.shape[1]
    pair_slots = boundary_blocks.shape[2]
    slots = ndom * pair_slots
    grows = rows * nhead
    bsize = grows // nblk
    score_scale = 1.0 / math.sqrt(depth)

    xf = features.astype(f32)
    inv = lax.rsqrt(jnp.mean(xf * xf, axis=1, keepdims=True) + EPS)
    normed = xf * inv
    hidden = (normed * norm_gain).astype(bf16)
    w_split = w_qkv.reshape(width, 3, nhead, hwide).transpose(2, 0, 1, 3)
    w_q = w_split[:, :, 0]
    w_kv = w_split[:, :, 1:].reshape(nhead, width, 2 * hwide)
    w_out_heads = w_out.reshape(nhead, hwide, width)
    kv_own = jnp.einsum("rd,hdc->hrc", hidden, w_kv, preferred_element_type=f32).astype(bf16)
    kv = lax.all_to_all(kv_own, "head", split_axis=0, concat_axis=0, tiled=True).reshape(
        nblk, bsize, 2 * hwide
    )
    q_own = jnp.einsum("rd,hdc->hrc", hidden, w_q, preferred_element_type=f32).astype(bf16)
    d_attn = jnp.einsum("rf,hef->hre", grad_y, w_out_heads, preferred_element_type=f32).astype(bf16)

    send_ids = boundary_blocks[0].reshape(slots)
    outgoing = jnp.take(kv, send_ids, axis=0, mode="clip")
    outgoing, q_own, d_attn = lax.optimization_barrier((outgoing, q_own, d_attn))
    queries = head_exchange(q_own, "head").reshape(nblk, bsize, hwide)
    d_group = head_exchange(d_attn, "head").reshape(nblk, bsize, hwide)
    pool = lax.all_to_all(
        outgoing.reshape(ndom, pair_slots * bsize, 2 * hwide),
        "dom",
        split_axis=0,
        concat_axis=0,
        tiled=True,
    ).reshape(slots, bsize, 2 * hwide)
    slot_alive = (jnp.arange(pair_slots, dtype=jnp.int32)[None, :] < boundary_count).reshape(slots)
    remote_alive = jnp.take(slot_alive, remote_keys, axis=0, mode="clip")
    bias_far = jnp.where(remote_alive, 0.0, -jnp.inf).astype(f32)
    bias = jnp.concatenate([jnp.zeros((nblk, near_count), f32), bias_far], axis=1)
    bias = jnp.repeat(bias, bsize, axis=1)

    o, d_q, acc, slot_grads = fused_attention(
        local_keys.reshape(-1), remote_keys.reshape(-1), queries, kv, d_group, pool, bias,
        score_scale,
    )

    attn = head_exchange(o.reshape(nhead, rows, hwide), "head")
    mixed_out = (
        xf + jnp.einsum("hre,hef->rf", attn, w_out_heads, preferred_element_type=f32)
    ).astype(bf16)
    d_rows_q = head_exchange(d_q.reshape(nhead, rows, hwide), "head")
    d_hidden_q = jnp.einsum("hrc,hdc->rd", d_rows_q, w_q, preferred_element_type=f32)

    returned = lax.all_to_all(
        slot_grads.reshape(ndom, pair_slots * 2 * hwide, bsize),
        "dom",
        split_axis=0,
        concat_axis=0,
        tiled=True,
    ).reshape(slots, 2 * hwide, bsize)
    d_kv = finish_grads(send_ids, acc, returned)
    d_rows = lax.all_to_all(
        d_kv.reshape(nhead, rows, 2 * hwide), "head", split_axis=0, concat_axis=0, tiled=True
    )
    d_hidden = d_hidden_q + jnp.einsum("hrc,hdc->rd", d_rows, w_kv, preferred_element_type=f32)
    d_normed = d_hidden * norm_gain
    d_input = inv * (d_normed - normed * jnp.mean(d_normed * normed, axis=1, keepdims=True))
    grad_x = (grad_y.astype(f32) + d_input).astype(bf16)
    return (mixed_out, grad_x)


def solution(mesh):
    return jax.shard_map(
        local,
        mesh=mesh,
        in_specs=(
            P(("dom", "head"), None),
            P(),
            P(),
            P(),
            P(("dom", "head"), None),
            P("dom", None),
            P("dom", None),
            P("dom", None, None),
            P(None, "dom"),
        ),
        out_specs=(P(("dom", "head"), None), P(("dom", "head"), None)),
        check_vma=False,
    )
```

```python
import math

import jax
import jax.numpy as jnp
from jax import lax
from jax.experimental import pallas as pl
from jax.experimental.pallas import tpu as pltpu
from jax.sharding import PartitionSpec as P

HEADS = 8
EPS = 1e-05


def load_blocks(kv_ref, pool_ref, ids_l, ids_r, cols):
    return jnp.concatenate(
        [kv_ref[i, :, cols] for i in ids_l] + [pool_ref[i, :, cols] for i in ids_r], axis=0
    )


def remote_kernel(
    lk_ref, rk_ref, q_ref, kv_ref, do_ref, pool_ref, bias_ref, o_ref, dq_ref, stats_ref,
    slot_ref, slot_acc, *, near, far, bsize, depth, scale
):
    f32 = jnp.float32
    bf16 = jnp.bfloat16
    nq = q_ref.shape[0]
    slot_acc[...] = jnp.zeros(slot_acc.shape, f32)
    kcols = pl.ds(0, depth)
    vcols = pl.ds(depth, depth)
    nt = (((1,), (1,)), ((), ()))
    split = near * bsize

    def body(b, carry):
        q = q_ref[b]
        do = do_ref[b]
        ids_l = [lk_ref[b * near + i] for i in range(near)]
        ids_r = [rk_ref[b * far + i] for i in range(far)]
        keys = load_blocks(kv_ref, pool_ref, ids_l, ids_r, kcols)
        vals = load_blocks(kv_ref, pool_ref, ids_l, ids_r, vcols)
        q_s = q * scale
        do_s = do * scale
        s = lax.dot_general(q_s, keys, nt, preferred_element_type=f32)
        s = s + bias_ref[pl.ds(b, 1), :]
        top = jnp.max(s, axis=1, keepdims=True)
        expo = jnp.exp(s - top)
        total = jnp.sum(expo, axis=1, keepdims=True)
        rtot = 1.0 / total
        w = (expo * rtot).astype(bf16)
        o = jnp.dot(w, vals, preferred_element_type=f32).astype(bf16)
        o_ref[b] = o
        delta = jnp.sum(do_s.astype(f32) * o.astype(f32), axis=1, keepdims=True)
        stats_ref[b] = jnp.concatenate([top, rtot, delta], axis=1)
        keys_r = keys[split:]
        vals_r = vals[split:]
        w_r = w[:, split:]
        dw = lax.dot_general(do_s, vals_r, nt, preferred_element_type=f32)
        ds = (w_r.astype(f32) * (dw - delta)).astype(bf16)
        dq_ref[b] = jnp.dot(ds, keys_r, preferred_element_type=f32)
        dk_t = jnp.dot(q.T, ds, preferred_element_type=f32)
        dv_t = jnp.dot(do.T, w_r, preferred_element_type=f32)
        dkv_t = jnp.concatenate([dk_t, dv_t], axis=0)
        for i in range(far):
            part = dkv_t[:, i * bsize:(i + 1) * bsize]
            slot_acc[ids_r[i]] = slot_acc[ids_r[i]] + part
        return carry

    lax.fori_loop(0, nq, body, 0, unroll=4)
    slot_ref[...] = slot_acc[...].astype(bf16)


def local_kernel(
    lk_ref, q_ref, kv_ref, do_ref, stats_ref, dqr_ref, dq_ref, acc_ref,
    *, near, bsize, depth, scale
):
    f32 = jnp.float32
    bf16 = jnp.bfloat16
    nq = q_ref.shape[0]
    acc_ref[...] = jnp.zeros(acc_ref.shape, f32)
    kcols = pl.ds(0, depth)
    vcols = pl.ds(depth, depth)
    nt = (((1,), (1,)), ((), ()))

    def body(b, carry):
        q = q_ref[b]
        do = do_ref[b]
        ids_l = [lk_ref[b * near + i] for i in range(near)]
        keys = jnp.concatenate([kv_ref[i, :, kcols] for i in ids_l], axis=0)
        vals = jnp.concatenate([kv_ref[i, :, vcols] for i in ids_l], axis=0)
        q_s = q * scale
        do_s = do * scale
        stats = stats_ref[b]
        top = stats[:, 0:1]
        rtot = stats[:, 1:2]
        delta = stats[:, 2:3]
        s = lax.dot_general(q_s, keys, nt, preferred_element_type=f32)
        w = (jnp.exp(s - top) * rtot).astype(bf16)
        dw = lax.dot_general(do_s, vals, nt, preferred_element_type=f32)
        ds = (w.astype(f32) * (dw - delta)).astype(bf16)
        dq = dqr_ref[b] + jnp.dot(ds, keys, preferred_element_type=f32)
        dq_ref[b] = dq.astype(bf16)
        dk_t = jnp.dot(q.T, ds, preferred_element_type=f32)
        dv_t = jnp.dot(do.T, w, preferred_element_type=f32)
        dkv_t = jnp.concatenate([dk_t, dv_t], axis=0)
        for i in range(near):
            part = dkv_t[:, i * bsize:(i + 1) * bsize]
            acc_ref[ids_l[i]] = acc_ref[ids_l[i]] + part
        return carry

    lax.fori_loop(0, nq, body, 0, unroll=4)


def fused_attention(local_ids, remote_ids, q, kv, d_out, pool, bias, scale):
    nq, bsize, depth = d_out.shape
    near = local_ids.size // nq
    far = remote_ids.size // nq
    npool = pool.shape[0]
    f32 = jnp.float32
    smem = pl.BlockSpec(memory_space=pltpu.SMEM)
    vmem = pl.BlockSpec(memory_space=pltpu.VMEM)
    kv_t = (2 * depth, bsize)
    params = pltpu.CompilerParams(vmem_limit_bytes=60 * 1024 * 1024)
    o, dq_r, stats, slot = pl.pallas_call(
        lambda *refs: remote_kernel(
            *refs, near=near, far=far, bsize=bsize, depth=depth, scale=scale
        ),
        out_shape=(
            jax.ShapeDtypeStruct((nq, bsize, depth), jnp.bfloat16),
            jax.ShapeDtypeStruct((nq, bsize, depth), f32),
            jax.ShapeDtypeStruct((nq, bsize, 3), f32),
            jax.ShapeDtypeStruct((npool,) + kv_t, jnp.bfloat16),
        ),
        in_specs=[smem, smem] + [vmem] * 5,
        out_specs=(vmem, vmem, vmem, vmem),
        scratch_shapes=[pltpu.VMEM((npool,) + kv_t, f32)],
        compiler_params=params,
    )(local_ids, remote_ids, q, kv, d_out, pool, bias)
    dq, acc = pl.pallas_call(
        lambda *refs: local_kernel(*refs, near=near, bsize=bsize, depth=depth, scale=scale),
        out_shape=(
            jax.ShapeDtypeStruct((nq, bsize, depth), jnp.bfloat16),
            jax.ShapeDtypeStruct((nq,) + kv_t, f32),
        ),
        in_specs=[smem] + [vmem] * 5,
        out_specs=(vmem, vmem),
        compiler_params=params,
    )(local_ids, q, kv, d_out, stats, dq_r)
    return o, dq, acc, slot


def finish_kernel(ids_ref, acc_ref, ret_ref, out_ref, total_ref):
    total_ref[...] = acc_ref[...]

    def add_slot(j, carry):
        i = ids_ref[j]
        total_ref[i] = total_ref[i] + ret_ref[j].astype(jnp.float32)
        return carry

    lax.fori_loop(0, ret_ref.shape[0], add_slot, 0, unroll=8)

    def emit(b, carry):
        out_ref[b] = total_ref[b].T.astype(jnp.bfloat16)
        return carry

    lax.fori_loop(0, acc_ref.shape[0], emit, 0, unroll=4)


def finish_grads(send_ids, acc, returned):
    nq, kvw, bsize = acc.shape
    smem = pl.BlockSpec(memory_space=pltpu.SMEM)
    vmem = pl.BlockSpec(memory_space=pltpu.VMEM)
    return pl.pallas_call(
        finish_kernel,
        out_shape=jax.ShapeDtypeStruct((nq, bsize, kvw), jnp.bfloat16),
        in_specs=[smem, vmem, vmem],
        out_specs=vmem,
        scratch_shapes=[pltpu.VMEM(acc.shape, jnp.float32)],
        compiler_params=pltpu.CompilerParams(vmem_limit_bytes=60 * 1024 * 1024),
    )(send_ids, acc, returned)


def head_exchange(x, axis):
    n = x.shape[0]
    me = lax.axis_index(axis)
    out = x
    for k in range(1, n):
        perm = [(i, (i + k) % n) for i in range(n)]
        part = lax.dynamic_index_in_dim(x, (me + k) % n, 0, keepdims=True)
        got = lax.ppermute(part, axis, perm)
        out = lax.dynamic_update_index_in_dim(out, got, (me + n - k) % n, 0)
    return out


def local(
    features,
    norm_gain,
    w_qkv,
    w_out,
    grad_y,
    local_keys,
    remote_keys,
    boundary_blocks,
    boundary_count,
):
    f32 = jnp.float32
    bf16 = jnp.bfloat16
    nhead = lax.axis_size("head")
    rows, width = features.shape
    per = HEADS // nhead
    depth = width // HEADS
    hwide = per * depth
    nblk, near_count = local_keys.shape
    far_count = remote_keys.shape[1]
    ndom = boundary_blocks.shape[1]
    pair_slots = boundary_blocks.shape[2]
    slots = ndom * pair_slots
    grows = rows * nhead
    bsize = grows // nblk
    score_scale = 1.0 / math.sqrt(depth)

    xf = features.astype(f32)
    inv = lax.rsqrt(jnp.mean(xf * xf, axis=1, keepdims=True) + EPS)
    normed = xf * inv
    hidden = (normed * norm_gain).astype(bf16)
    w_split = w_qkv.reshape(width, 3, nhead, hwide).transpose(2, 0, 1, 3)
    w_q = w_split[:, :, 0]
    w_kv = w_split[:, :, 1:].reshape(nhead, width, 2 * hwide)
    w_out_heads = w_out.reshape(nhead, hwide, width)
    kv_own = jnp.einsum("rd,hdc->hrc", hidden, w_kv, preferred_element_type=f32).astype(bf16)
    kv = lax.all_to_all(kv_own, "head", split_axis=0, concat_axis=0, tiled=True).reshape(
        nblk, bsize, 2 * hwide
    )
    q_own = jnp.einsum("rd,hdc->hrc", hidden, w_q, preferred_element_type=f32).astype(bf16)
    d_attn = jnp.einsum("rf,hef->hre", grad_y, w_out_heads, preferred_element_type=f32).astype(bf16)

    send_ids = boundary_blocks[0].reshape(slots)
    outgoing = jnp.take(kv, send_ids, axis=0, mode="clip")
    outgoing, q_own, d_attn = lax.optimization_barrier((outgoing, q_own, d_attn))
    queries = head_exchange(q_own, "head").reshape(nblk, bsize, hwide)
    d_group = head_exchange(d_attn, "head").reshape(nblk, bsize, hwide)
    pool = lax.all_to_all(
        outgoing.reshape(ndom, pair_slots * bsize, 2 * hwide),
        "dom",
        split_axis=0,
        concat_axis=0,
        tiled=True,
    ).reshape(slots, bsize, 2 * hwide)
    slot_alive = (jnp.arange(pair_slots, dtype=jnp.int32)[None, :] < boundary_count).reshape(slots)
    remote_alive = jnp.take(slot_alive, remote_keys, axis=0, mode="clip")
    bias_far = jnp.where(remote_alive, 0.0, -jnp.inf).astype(f32)
    bias = jnp.concatenate([jnp.zeros((nblk, near_count), f32), bias_far], axis=1)
    bias = jnp.repeat(bias, bsize, axis=1)

    o, d_q, acc, slot_grads = fused_attention(
        local_keys.reshape(-1), remote_keys.reshape(-1), queries, kv, d_group, pool, bias,
        score_scale,
    )

    attn = head_exchange(o.reshape(nhead, rows, hwide), "head")
    mixed_out = (
        xf + jnp.einsum("hre,hef->rf", attn, w_out_heads, preferred_element_type=f32)
    ).astype(bf16)
    d_rows_q = head_exchange(d_q.reshape(nhead, rows, hwide), "head")
    d_hidden_q = jnp.einsum("hrc,hdc->rd", d_rows_q, w_q, preferred_element_type=f32)

    returned = lax.all_to_all(
        slot_grads.reshape(ndom, pair_slots * 2 * hwide, bsize),
        "dom",
        split_axis=0,
        concat_axis=0,
        tiled=True,
    ).reshape(slots, 2 * hwide, bsize)
    d_kv = finish_grads(send_ids, acc, returned)
    d_rows = lax.all_to_all(
        d_kv.reshape(nhead, rows, 2 * hwide), "head", split_axis=0, concat_axis=0, tiled=True
    )
    d_hidden = d_hidden_q + jnp.einsum("hrc,hdc->rd", d_rows, w_kv, preferred_element_type=f32)
    d_normed = d_hidden * norm_gain
    d_input = inv * (d_normed - normed * jnp.mean(d_normed * normed, axis=1, keepdims=True))
    grad_x = (grad_y.astype(f32) + d_input).astype(bf16)
    return (mixed_out, grad_x)


def solution(mesh):
    return jax.shard_map(
        local,
        mesh=mesh,
        in_specs=(
            P(("dom", "head"), None),
            P(),
            P(),
            P(),
            P(("dom", "head"), None),
            P("dom", None),
            P("dom", None),
            P("dom", None, None),
            P(None, "dom"),
        ),
        out_specs=(P(("dom", "head"), None), P(("dom", "head"), None)),
        check_vma=False,
    )
```

```python
import math

import jax
import jax.numpy as jnp
from jax import lax
from jax.experimental import pallas as pl
from jax.experimental.pallas import tpu as pltpu
from jax.sharding import PartitionSpec as P

HEADS = 8
EPS = 1e-05


def load_blocks(kv_ref, pool_ref, ids_l, ids_r, cols):
    return jnp.concatenate(
        [kv_ref[i, :, cols] for i in ids_l] + [pool_ref[i, :, cols] for i in ids_r], axis=0
    )


def column_to_row(col):
    n = col.shape[0]
    return jnp.broadcast_to(col, (n, n)).T[0:1, :]


def row_to_column(row):
    n = row.shape[1]
    return jnp.broadcast_to(row, (n, n)).T[:, 0:1]


def remote_kernel(
    lk_ref, rk_ref, q_ref, kv_ref, do_ref, pool_ref, bias_ref, o_ref, dq_ref, stats_ref,
    slot_ref, slot_acc, *, near, far, bsize, depth, scale
):
    f32 = jnp.float32
    bf16 = jnp.bfloat16
    nq = q_ref.shape[0]
    slot_acc[...] = jnp.zeros(slot_acc.shape, f32)
    kcols = pl.ds(0, depth)
    vcols = pl.ds(depth, depth)
    nt = (((1,), (1,)), ((), ()))
    split = near * bsize

    def body(b, carry):
        q = q_ref[b]
        do = do_ref[b]
        ids_l = [lk_ref[b * near + i] for i in range(near)]
        ids_r = [rk_ref[b * far + i] for i in range(far)]
        keys = load_blocks(kv_ref, pool_ref, ids_l, ids_r, kcols)
        vals = load_blocks(kv_ref, pool_ref, ids_l, ids_r, vcols)
        q_s = q * scale
        do_s = do * scale
        s = lax.dot_general(q_s, keys, nt, preferred_element_type=f32)
        s = s + bias_ref[pl.ds(b, 1), :]
        top = jnp.max(s, axis=1, keepdims=True)
        expo = jnp.exp(s - top)
        total = jnp.sum(expo, axis=1, keepdims=True)
        rtot = 1.0 / total
        w = (expo * rtot).astype(bf16)
        o = jnp.dot(w, vals, preferred_element_type=f32).astype(bf16)
        o_ref[b] = o
        delta = jnp.sum(do_s.astype(f32) * o.astype(f32), axis=1, keepdims=True)
        stats_ref[b] = jnp.concatenate(
            [column_to_row(top), column_to_row(rtot), column_to_row(delta)], axis=0
        )
        keys_r = keys[split:]
        vals_r = vals[split:]
        w_r = w[:, split:]
        dw = lax.dot_general(do_s, vals_r, nt, preferred_element_type=f32)
        ds = (w_r.astype(f32) * (dw - delta)).astype(bf16)
        dq_ref[b] = jnp.dot(ds, keys_r, preferred_element_type=f32)
        dk_t = jnp.dot(q.T, ds, preferred_element_type=f32)
        dv_t = jnp.dot(do.T, w_r, preferred_element_type=f32)
        dkv_t = jnp.concatenate([dk_t, dv_t], axis=0)
        for i in range(far):
            part = dkv_t[:, i * bsize:(i + 1) * bsize]
            slot_acc[ids_r[i]] = slot_acc[ids_r[i]] + part
        return carry

    lax.fori_loop(0, nq, body, 0, unroll=8)
    slot_ref[...] = slot_acc[...].astype(bf16)


def local_kernel(
    lk_ref, q_ref, kv_ref, do_ref, stats_ref, dqr_ref, dq_ref, acc_ref,
    *, near, bsize, depth, scale
):
    f32 = jnp.float32
    bf16 = jnp.bfloat16
    nq = q_ref.shape[0]
    acc_ref[...] = jnp.zeros(acc_ref.shape, f32)
    kcols = pl.ds(0, depth)
    vcols = pl.ds(depth, depth)
    nt = (((1,), (1,)), ((), ()))

    def body(b, carry):
        q = q_ref[b]
        do = do_ref[b]
        ids_l = [lk_ref[b * near + i] for i in range(near)]
        keys = jnp.concatenate([kv_ref[i, :, kcols] for i in ids_l], axis=0)
        vals = jnp.concatenate([kv_ref[i, :, vcols] for i in ids_l], axis=0)
        q_s = q * scale
        do_s = do * scale
        stats = stats_ref[b]
        top = row_to_column(stats[0:1, :])
        rtot = row_to_column(stats[1:2, :])
        delta = row_to_column(stats[2:3, :])
        s = lax.dot_general(q_s, keys, nt, preferred_element_type=f32)
        w = (jnp.exp(s - top) * rtot).astype(bf16)
        dw = lax.dot_general(do_s, vals, nt, preferred_element_type=f32)
        ds = (w.astype(f32) * (dw - delta)).astype(bf16)
        dq = dqr_ref[b] + jnp.dot(ds, keys, preferred_element_type=f32)
        dq_ref[b] = dq.astype(bf16)
        dk_t = jnp.dot(q.T, ds, preferred_element_type=f32)
        dv_t = jnp.dot(do.T, w, preferred_element_type=f32)
        dkv_t = jnp.concatenate([dk_t, dv_t], axis=0)
        for i in range(near):
            part = dkv_t[:, i * bsize:(i + 1) * bsize]
            acc_ref[ids_l[i]] = acc_ref[ids_l[i]] + part
        return carry

    lax.fori_loop(0, nq, body, 0, unroll=4)


def fused_attention(local_ids, remote_ids, q, kv, d_out, pool, bias, scale):
    nq, bsize, depth = d_out.shape
    near = local_ids.size // nq
    far = remote_ids.size // nq
    npool = pool.shape[0]
    f32 = jnp.float32
    smem = pl.BlockSpec(memory_space=pltpu.SMEM)
    vmem = pl.BlockSpec(memory_space=pltpu.VMEM)
    kv_t = (2 * depth, bsize)
    params = pltpu.CompilerParams(vmem_limit_bytes=60 * 1024 * 1024)
    o, dq_r, stats, slot = pl.pallas_call(
        lambda *refs: remote_kernel(
            *refs, near=near, far=far, bsize=bsize, depth=depth, scale=scale
        ),
        out_shape=(
            jax.ShapeDtypeStruct((nq, bsize, depth), jnp.bfloat16),
            jax.ShapeDtypeStruct((nq, bsize, depth), f32),
            jax.ShapeDtypeStruct((nq, 3, bsize), f32),
            jax.ShapeDtypeStruct((npool,) + kv_t, jnp.bfloat16),
        ),
        in_specs=[smem, smem] + [vmem] * 5,
        out_specs=(vmem, vmem, vmem, vmem),
        scratch_shapes=[pltpu.VMEM((npool,) + kv_t, f32)],
        compiler_params=params,
    )(local_ids, remote_ids, q, kv, d_out, pool, bias)
    dq, acc = pl.pallas_call(
        lambda *refs: local_kernel(*refs, near=near, bsize=bsize, depth=depth, scale=scale),
        out_shape=(
            jax.ShapeDtypeStruct((nq, bsize, depth), jnp.bfloat16),
            jax.ShapeDtypeStruct((nq,) + kv_t, f32),
        ),
        in_specs=[smem] + [vmem] * 5,
        out_specs=(vmem, vmem),
        compiler_params=params,
    )(local_ids, q, kv, d_out, stats, dq_r)
    return o, dq, acc, slot


def finish_kernel(ids_ref, acc_ref, ret_ref, out_ref, total_ref):
    total_ref[...] = acc_ref[...]

    def add_slot(j, carry):
        i = ids_ref[j]
        total_ref[i] = total_ref[i] + ret_ref[j].astype(jnp.float32)
        return carry

    lax.fori_loop(0, ret_ref.shape[0], add_slot, 0, unroll=8)

    def emit(b, carry):
        out_ref[b] = total_ref[b].T.astype(jnp.bfloat16)
        return carry

    lax.fori_loop(0, acc_ref.shape[0], emit, 0, unroll=4)


def finish_grads(send_ids, acc, returned):
    nq, kvw, bsize = acc.shape
    smem = pl.BlockSpec(memory_space=pltpu.SMEM)
    vmem = pl.BlockSpec(memory_space=pltpu.VMEM)
    return pl.pallas_call(
        finish_kernel,
        out_shape=jax.ShapeDtypeStruct((nq, bsize, kvw), jnp.bfloat16),
        in_specs=[smem, vmem, vmem],
        out_specs=vmem,
        scratch_shapes=[pltpu.VMEM(acc.shape, jnp.float32)],
        compiler_params=pltpu.CompilerParams(vmem_limit_bytes=60 * 1024 * 1024),
    )(send_ids, acc, returned)


def head_exchange(x, axis):
    n = x.shape[0]
    me = lax.axis_index(axis)
    out = x
    for k in range(1, n):
        perm = [(i, (i + k) % n) for i in range(n)]
        part = lax.dynamic_index_in_dim(x, (me + k) % n, 0, keepdims=True)
        got = lax.ppermute(part, axis, perm)
        out = lax.dynamic_update_index_in_dim(out, got, (me + n - k) % n, 0)
    return out


def local(
    features,
    norm_gain,
    w_qkv,
    w_out,
    grad_y,
    local_keys,
    remote_keys,
    boundary_blocks,
    boundary_count,
):
    f32 = jnp.float32
    bf16 = jnp.bfloat16
    nhead = lax.axis_size("head")
    rows, width = features.shape
    per = HEADS // nhead
    depth = width // HEADS
    hwide = per * depth
    nblk, near_count = local_keys.shape
    far_count = remote_keys.shape[1]
    ndom = boundary_blocks.shape[1]
    pair_slots = boundary_blocks.shape[2]
    slots = ndom * pair_slots
    grows = rows * nhead
    bsize = grows // nblk
    score_scale = 1.0 / math.sqrt(depth)

    xf = features.astype(f32)
    inv = lax.rsqrt(jnp.mean(xf * xf, axis=1, keepdims=True) + EPS)
    normed = xf * inv
    hidden = (normed * norm_gain).astype(bf16)
    w_q = w_qkv[:, :width].reshape(width, nhead, hwide).transpose(1, 0, 2)
    w_kv = (
        w_qkv[:, width:]
        .reshape(width, 2, nhead, hwide)
        .transpose(2, 0, 1, 3)
        .reshape(nhead, width, 2 * hwide)
    )
    w_out_heads = w_out.reshape(nhead, hwide, width)
    kv_own = jnp.einsum("rd,hdc->hrc", hidden, w_kv, preferred_element_type=f32).astype(bf16)
    kv = lax.all_to_all(kv_own, "head", split_axis=0, concat_axis=0, tiled=True).reshape(
        nblk, bsize, 2 * hwide
    )
    q_own = jnp.einsum("rd,hdc->hrc", hidden, w_q, preferred_element_type=f32).astype(bf16)
    d_attn = jnp.einsum("rf,hef->hre", grad_y, w_out_heads, preferred_element_type=f32).astype(bf16)

    send_ids = boundary_blocks[0].reshape(slots)
    outgoing = jnp.take(kv, send_ids, axis=0, mode="clip")
    outgoing, q_own, d_attn = lax.optimization_barrier((outgoing, q_own, d_attn))
    queries = head_exchange(q_own, "head").reshape(nblk, bsize, hwide)
    d_group = head_exchange(d_attn, "head").reshape(nblk, bsize, hwide)
    pool = lax.all_to_all(
        outgoing.reshape(ndom, pair_slots * bsize, 2 * hwide),
        "dom",
        split_axis=0,
        concat_axis=0,
        tiled=True,
    ).reshape(slots, bsize, 2 * hwide)
    slot_alive = (jnp.arange(pair_slots, dtype=jnp.int32)[None, :] < boundary_count).reshape(slots)
    remote_alive = jnp.take(slot_alive, remote_keys, axis=0, mode="clip")
    bias_far = jnp.where(remote_alive, 0.0, -jnp.inf).astype(f32)
    bias = jnp.concatenate([jnp.zeros((nblk, near_count), f32), bias_far], axis=1)
    bias = jnp.repeat(bias, bsize, axis=1)

    o, d_q, acc, slot_grads = fused_attention(
        local_keys.reshape(-1), remote_keys.reshape(-1), queries, kv, d_group, pool, bias,
        score_scale,
    )

    attn = head_exchange(o.reshape(nhead, rows, hwide), "head")
    mixed_out = (
        xf + jnp.einsum("hre,hef->rf", attn, w_out_heads, preferred_element_type=f32)
    ).astype(bf16)
    d_rows_q = head_exchange(d_q.reshape(nhead, rows, hwide), "head")
    d_hidden_q = jnp.einsum("hrc,hdc->rd", d_rows_q, w_q, preferred_element_type=f32)

    returned = lax.all_to_all(
        slot_grads.reshape(ndom, pair_slots * 2 * hwide, bsize),
        "dom",
        split_axis=0,
        concat_axis=0,
        tiled=True,
    ).reshape(slots, 2 * hwide, bsize)
    d_kv = finish_grads(send_ids, acc, returned)
    d_rows = lax.all_to_all(
        d_kv.reshape(nhead, rows, 2 * hwide), "head", split_axis=0, concat_axis=0, tiled=True
    )
    d_hidden = d_hidden_q + jnp.einsum("hrc,hdc->rd", d_rows, w_kv, preferred_element_type=f32)
    d_normed = d_hidden * norm_gain
    d_input = inv * (d_normed - normed * jnp.mean(d_normed * normed, axis=1, keepdims=True))
    grad_x = (grad_y.astype(f32) + d_input).astype(bf16)
    return (mixed_out, grad_x)


def solution(mesh):
    return jax.shard_map(
        local,
        mesh=mesh,
        in_specs=(
            P(("dom", "head"), None),
            P(),
            P(),
            P(),
            P(("dom", "head"), None),
            P("dom", None),
            P("dom", None),
            P("dom", None, None),
            P(None, "dom"),
        ),
        out_specs=(P(("dom", "head"), None), P(("dom", "head"), None)),
        check_vma=False,
    )
```

```python
import math

import jax
import jax.numpy as jnp
from jax import lax
from jax.experimental import pallas as pl
from jax.experimental.pallas import tpu as pltpu
from jax.sharding import PartitionSpec as P

HEADS = 8
EPS = 1e-05


def load_blocks(kv_ref, pool_ref, ids_l, ids_r, cols):
    return jnp.concatenate(
        [kv_ref[i, :, cols] for i in ids_l] + [pool_ref[i, :, cols] for i in ids_r], axis=0
    )


def column_to_row(col):
    n = col.shape[0]
    return jnp.broadcast_to(col, (n, n)).T[0:1, :]


def row_to_column(row):
    n = row.shape[1]
    return jnp.broadcast_to(row, (n, n)).T[:, 0:1]


def remote_kernel(
    lk_ref, rk_ref, q_ref, kv_ref, do_ref, pool_ref, bias_ref, o_ref, dq_ref, stats_ref,
    slot_ref, slot_acc, *, near, far, bsize, depth, scale
):
    f32 = jnp.float32
    bf16 = jnp.bfloat16
    nq = q_ref.shape[0]
    step = pl.program_id(0)

    @pl.when(step == 0)
    def _():
        slot_acc[...] = jnp.zeros(slot_acc.shape, f32)

    kcols = pl.ds(0, depth)
    vcols = pl.ds(depth, depth)
    nt = (((1,), (1,)), ((), ()))
    split = near * bsize

    def body(b, carry):
        g = step * nq + b
        q = q_ref[b]
        do = do_ref[b]
        ids_l = [lk_ref[g * near + i] for i in range(near)]
        ids_r = [rk_ref[g * far + i] for i in range(far)]
        keys = load_blocks(kv_ref, pool_ref, ids_l, ids_r, kcols)
        vals = load_blocks(kv_ref, pool_ref, ids_l, ids_r, vcols)
        q_s = q * scale
        do_s = do * scale
        s = lax.dot_general(q_s, keys, nt, preferred_element_type=f32)
        s = s + bias_ref[pl.ds(b, 1), :]
        top = jnp.max(s, axis=1, keepdims=True)
        expo = jnp.exp(s - top)
        total = jnp.sum(expo, axis=1, keepdims=True)
        rtot = 1.0 / total
        w = (expo * rtot).astype(bf16)
        o = jnp.dot(w, vals, preferred_element_type=f32).astype(bf16)
        o_ref[b] = o
        delta = jnp.sum(do_s.astype(f32) * o.astype(f32), axis=1, keepdims=True)
        stats_ref[b] = jnp.concatenate(
            [column_to_row(top), column_to_row(rtot), column_to_row(delta)], axis=0
        )
        keys_r = keys[split:]
        vals_r = vals[split:]
        w_r = w[:, split:]
        dw = lax.dot_general(do_s, vals_r, nt, preferred_element_type=f32)
        ds = (w_r.astype(f32) * (dw - delta)).astype(bf16)
        dq_ref[b] = jnp.dot(ds, keys_r, preferred_element_type=f32)
        dk_t = jnp.dot(q.T, ds, preferred_element_type=f32)
        dv_t = jnp.dot(do.T, w_r, preferred_element_type=f32)
        dkv_t = jnp.concatenate([dk_t, dv_t], axis=0)
        for i in range(far):
            part = dkv_t[:, i * bsize:(i + 1) * bsize]
            slot_acc[ids_r[i]] = slot_acc[ids_r[i]] + part
        return carry

    lax.fori_loop(0, nq, body, 0, unroll=4)

    @pl.when(step == pl.num_programs(0) - 1)
    def _():
        slot_ref[...] = slot_acc[...].astype(bf16)


def local_kernel(
    lk_ref, q_ref, kv_ref, do_ref, stats_ref, dqr_ref, dq_ref, acc_ref,
    *, near, bsize, depth, scale
):
    f32 = jnp.float32
    bf16 = jnp.bfloat16
    nq = q_ref.shape[0]
    acc_ref[...] = jnp.zeros(acc_ref.shape, f32)
    kcols = pl.ds(0, depth)
    vcols = pl.ds(depth, depth)
    nt = (((1,), (1,)), ((), ()))

    def body(b, carry):
        q = q_ref[b]
        do = do_ref[b]
        ids_l = [lk_ref[b * near + i] for i in range(near)]
        keys = jnp.concatenate([kv_ref[i, :, kcols] for i in ids_l], axis=0)
        vals = jnp.concatenate([kv_ref[i, :, vcols] for i in ids_l], axis=0)
        q_s = q * scale
        do_s = do * scale
        stats = stats_ref[b]
        top = row_to_column(stats[0:1, :])
        rtot = row_to_column(stats[1:2, :])
        delta = row_to_column(stats[2:3, :])
        s = lax.dot_general(q_s, keys, nt, preferred_element_type=f32)
        w = (jnp.exp(s - top) * rtot).astype(bf16)
        dw = lax.dot_general(do_s, vals, nt, preferred_element_type=f32)
        ds = (w.astype(f32) * (dw - delta)).astype(bf16)
        dq = dqr_ref[b] + jnp.dot(ds, keys, preferred_element_type=f32)
        dq_ref[b] = dq.astype(bf16)
        dk_t = jnp.dot(q.T, ds, preferred_element_type=f32)
        dv_t = jnp.dot(do.T, w, preferred_element_type=f32)
        dkv_t = jnp.concatenate([dk_t, dv_t], axis=0)
        for i in range(near):
            part = dkv_t[:, i * bsize:(i + 1) * bsize]
            acc_ref[ids_l[i]] = acc_ref[ids_l[i]] + part
        return carry

    lax.fori_loop(0, nq, body, 0, unroll=4)


def fused_attention(local_ids, remote_ids, q, kv, d_out, pool, bias, scale):
    nq, bsize, depth = d_out.shape
    near = local_ids.size // nq
    far = remote_ids.size // nq
    npool = pool.shape[0]
    f32 = jnp.float32
    smem = pl.BlockSpec(memory_space=pltpu.SMEM)
    vmem = pl.BlockSpec(memory_space=pltpu.VMEM)
    kv_t = (2 * depth, bsize)
    params = pltpu.CompilerParams(vmem_limit_bytes=60 * 1024 * 1024)
    per_step = 8
    blk = lambda *shape: pl.BlockSpec((per_step,) + shape, lambda i: (i,) + (0,) * len(shape))
    whole = lambda a: pl.BlockSpec(a.shape, lambda i: (0,) * a.ndim)
    o, dq_r, stats, slot = pl.pallas_call(
        lambda *refs: remote_kernel(
            *refs, near=near, far=far, bsize=bsize, depth=depth, scale=scale
        ),
        grid=(nq // per_step,),
        out_shape=(
            jax.ShapeDtypeStruct((nq, bsize, depth), jnp.bfloat16),
            jax.ShapeDtypeStruct((nq, bsize, depth), f32),
            jax.ShapeDtypeStruct((nq, 3, bsize), f32),
            jax.ShapeDtypeStruct((npool,) + kv_t, jnp.bfloat16),
        ),
        in_specs=[
            smem, smem, blk(bsize, depth), whole(kv), blk(bsize, depth), whole(pool),
            pl.BlockSpec((per_step, bias.shape[1]), lambda i: (i, 0)),
        ],
        out_specs=(
            blk(bsize, depth), blk(bsize, depth), blk(3, bsize),
            pl.BlockSpec((npool,) + kv_t, lambda i: (0, 0, 0)),
        ),
        scratch_shapes=[pltpu.VMEM((npool,) + kv_t, f32)],
        compiler_params=pltpu.CompilerParams(
            dimension_semantics=("arbitrary",), vmem_limit_bytes=60 * 1024 * 1024
        ),
    )(local_ids, remote_ids, q, kv, d_out, pool, bias)
    dq, acc = pl.pallas_call(
        lambda *refs: local_kernel(*refs, near=near, bsize=bsize, depth=depth, scale=scale),
        out_shape=(
            jax.ShapeDtypeStruct((nq, bsize, depth), jnp.bfloat16),
            jax.ShapeDtypeStruct((nq,) + kv_t, f32),
        ),
        in_specs=[smem] + [vmem] * 5,
        out_specs=(vmem, vmem),
        compiler_params=params,
    )(local_ids, q, kv, d_out, stats, dq_r)
    return o, dq, acc, slot


def finish_kernel(ids_ref, acc_ref, ret_ref, out_ref, total_ref):
    total_ref[...] = acc_ref[...]

    def add_slot(j, carry):
        i = ids_ref[j]
        total_ref[i] = total_ref[i] + ret_ref[j].astype(jnp.float32)
        return carry

    lax.fori_loop(0, ret_ref.shape[0], add_slot, 0, unroll=8)

    def emit(b, carry):
        out_ref[b] = total_ref[b].T.astype(jnp.bfloat16)
        return carry

    lax.fori_loop(0, acc_ref.shape[0], emit, 0, unroll=4)


def finish_grads(send_ids, acc, returned):
    nq, kvw, bsize = acc.shape
    smem = pl.BlockSpec(memory_space=pltpu.SMEM)
    vmem = pl.BlockSpec(memory_space=pltpu.VMEM)
    return pl.pallas_call(
        finish_kernel,
        out_shape=jax.ShapeDtypeStruct((nq, bsize, kvw), jnp.bfloat16),
        in_specs=[smem, vmem, vmem],
        out_specs=vmem,
        scratch_shapes=[pltpu.VMEM(acc.shape, jnp.float32)],
        compiler_params=pltpu.CompilerParams(vmem_limit_bytes=60 * 1024 * 1024),
    )(send_ids, acc, returned)


def head_exchange(x, axis):
    n = x.shape[0]
    me = lax.axis_index(axis)
    out = x
    for k in range(1, n):
        perm = [(i, (i + k) % n) for i in range(n)]
        part = lax.dynamic_index_in_dim(x, (me + k) % n, 0, keepdims=True)
        got = lax.ppermute(part, axis, perm)
        out = lax.dynamic_update_index_in_dim(out, got, (me + n - k) % n, 0)
    return out


def local(
    features,
    norm_gain,
    w_qkv,
    w_out,
    grad_y,
    local_keys,
    remote_keys,
    boundary_blocks,
    boundary_count,
):
    f32 = jnp.float32
    bf16 = jnp.bfloat16
    nhead = lax.axis_size("head")
    rows, width = features.shape
    per = HEADS // nhead
    depth = width // HEADS
    hwide = per * depth
    nblk, near_count = local_keys.shape
    far_count = remote_keys.shape[1]
    ndom = boundary_blocks.shape[1]
    pair_slots = boundary_blocks.shape[2]
    slots = ndom * pair_slots
    grows = rows * nhead
    bsize = grows // nblk
    score_scale = 1.0 / math.sqrt(depth)

    xf = features.astype(f32)
    inv = lax.rsqrt(jnp.mean(xf * xf, axis=1, keepdims=True) + EPS)
    normed = xf * inv
    hidden = (normed * norm_gain).astype(bf16)
    w_q = w_qkv[:, :width].reshape(width, nhead, hwide).transpose(1, 0, 2)
    w_kv = (
        w_qkv[:, width:]
        .reshape(width, 2, nhead, hwide)
        .transpose(2, 0, 1, 3)
        .reshape(nhead, width, 2 * hwide)
    )
    w_out_heads = w_out.reshape(nhead, hwide, width)
    kv_own = jnp.einsum("rd,hdc->hrc", hidden, w_kv, preferred_element_type=f32).astype(bf16)
    kv = lax.all_to_all(kv_own, "head", split_axis=0, concat_axis=0, tiled=True).reshape(
        nblk, bsize, 2 * hwide
    )
    q_own = jnp.einsum("rd,hdc->hrc", hidden, w_q, preferred_element_type=f32).astype(bf16)
    d_attn = jnp.einsum("rf,hef->hre", grad_y, w_out_heads, preferred_element_type=f32).astype(bf16)

    send_ids = boundary_blocks[0].reshape(slots)
    outgoing = jnp.take(kv, send_ids, axis=0, mode="clip")
    outgoing, q_own, d_attn = lax.optimization_barrier((outgoing, q_own, d_attn))
    queries = head_exchange(q_own, "head").reshape(nblk, bsize, hwide)
    d_group = head_exchange(d_attn, "head").reshape(nblk, bsize, hwide)
    pool = lax.all_to_all(
        outgoing.reshape(ndom, pair_slots * bsize, 2 * hwide),
        "dom",
        split_axis=0,
        concat_axis=0,
        tiled=True,
    ).reshape(slots, bsize, 2 * hwide)
    slot_alive = (jnp.arange(pair_slots, dtype=jnp.int32)[None, :] < boundary_count).reshape(slots)
    remote_alive = jnp.take(slot_alive, remote_keys, axis=0, mode="clip")
    bias_far = jnp.where(remote_alive, 0.0, -jnp.inf).astype(f32)
    bias = jnp.concatenate([jnp.zeros((nblk, near_count), f32), bias_far], axis=1)
    bias = jnp.repeat(bias, bsize, axis=1)

    o, d_q, acc, slot_grads = fused_attention(
        local_keys.reshape(-1), remote_keys.reshape(-1), queries, kv, d_group, pool, bias,
        score_scale,
    )

    attn = head_exchange(o.reshape(nhead, rows, hwide), "head")
    mixed_out = (
        xf + jnp.einsum("hre,hef->rf", attn, w_out_heads, preferred_element_type=f32)
    ).astype(bf16)
    d_rows_q = head_exchange(d_q.reshape(nhead, rows, hwide), "head")
    d_hidden_q = jnp.einsum("hrc,hdc->rd", d_rows_q, w_q, preferred_element_type=f32)

    returned = lax.all_to_all(
        slot_grads.reshape(ndom, pair_slots * 2 * hwide, bsize),
        "dom",
        split_axis=0,
        concat_axis=0,
        tiled=True,
    ).reshape(slots, 2 * hwide, bsize)
    d_kv = finish_grads(send_ids, acc, returned)
    d_rows = lax.all_to_all(
        d_kv.reshape(nhead, rows, 2 * hwide), "head", split_axis=0, concat_axis=0, tiled=True
    )
    d_hidden = d_hidden_q + jnp.einsum("hrc,hdc->rd", d_rows, w_kv, preferred_element_type=f32)
    d_normed = d_hidden * norm_gain
    d_input = inv * (d_normed - normed * jnp.mean(d_normed * normed, axis=1, keepdims=True))
    grad_x = (grad_y.astype(f32) + d_input).astype(bf16)
    return (mixed_out, grad_x)


def solution(mesh):
    return jax.shard_map(
        local,
        mesh=mesh,
        in_specs=(
            P(("dom", "head"), None),
            P(),
            P(),
            P(),
            P(("dom", "head"), None),
            P("dom", None),
            P("dom", None),
            P("dom", None, None),
            P(None, "dom"),
        ),
        out_specs=(P(("dom", "head"), None), P(("dom", "head"), None)),
        check_vma=False,
    )
```

```python
import math

import jax
import jax.numpy as jnp
from jax import lax
from jax.experimental import pallas as pl
from jax.experimental.pallas import tpu as pltpu
from jax.sharding import PartitionSpec as P

HEADS = 8
EPS = 1e-05


def load_blocks(kv_ref, pool_ref, ids_l, ids_r, cols):
    return jnp.concatenate(
        [kv_ref[i, :, cols] for i in ids_l] + [pool_ref[i, :, cols] for i in ids_r], axis=0
    )


def column_to_row(col):
    n = col.shape[0]
    return jnp.broadcast_to(col, (n, n)).T[0:1, :]


def row_to_column(row):
    n = row.shape[1]
    return jnp.broadcast_to(row, (n, n)).T[:, 0:1]


def remote_kernel(
    lk_ref, rk_ref, q_ref, kv_ref, do_ref, pool_ref, bias_ref, o_ref, dq_ref, stats_ref,
    slot_ref, slot_acc, *, near, far, bsize, depth, scale
):
    f32 = jnp.float32
    bf16 = jnp.bfloat16
    nq = q_ref.shape[0]
    step = pl.program_id(0)

    @pl.when(step == 0)
    def _():
        slot_acc[...] = jnp.zeros(slot_acc.shape, f32)

    kcols = pl.ds(0, depth)
    vcols = pl.ds(depth, depth)
    nt = (((1,), (1,)), ((), ()))
    split = near * bsize

    def body(b, carry):
        g = step * nq + b
        q = q_ref[b]
        do = do_ref[b]
        ids_l = [lk_ref[g * near + i] for i in range(near)]
        ids_r = [rk_ref[g * far + i] for i in range(far)]
        keys = load_blocks(kv_ref, pool_ref, ids_l, ids_r, kcols)
        vals = load_blocks(kv_ref, pool_ref, ids_l, ids_r, vcols)
        q_s = q * scale
        do_s = do * scale
        s = lax.dot_general(q_s, keys, nt, preferred_element_type=f32)
        s = s + bias_ref[pl.ds(b, 1), :]
        top = jnp.max(s, axis=1, keepdims=True)
        expo = jnp.exp(s - top)
        total = jnp.sum(expo, axis=1, keepdims=True)
        rtot = 1.0 / total
        w = (expo * rtot).astype(bf16)
        o = jnp.dot(w, vals, preferred_element_type=f32).astype(bf16)
        o_ref[b] = o
        delta = jnp.sum(do_s.astype(f32) * o.astype(f32), axis=1, keepdims=True)
        stats_ref[b] = jnp.concatenate(
            [column_to_row(top), column_to_row(rtot), column_to_row(delta)], axis=0
        )
        keys_r = keys[split:]
        vals_r = vals[split:]
        w_r = w[:, split:]
        dw = lax.dot_general(do_s, vals_r, nt, preferred_element_type=f32)
        ds = (w_r.astype(f32) * (dw - delta)).astype(bf16)
        dq_ref[b] = jnp.dot(ds, keys_r, preferred_element_type=f32)
        dk_t = jnp.dot(q.T, ds, preferred_element_type=f32)
        dv_t = jnp.dot(do.T, w_r, preferred_element_type=f32)
        dkv_t = jnp.concatenate([dk_t, dv_t], axis=0)
        for i in range(far):
            part = dkv_t[:, i * bsize:(i + 1) * bsize]
            slot_acc[ids_r[i]] = slot_acc[ids_r[i]] + part
        return carry

    lax.fori_loop(0, nq, body, 0, unroll=4)

    @pl.when(step == pl.num_programs(0) - 1)
    def _():
        slot_ref[...] = slot_acc[...].astype(bf16)


def local_kernel(
    lk_ref, q_ref, kv_ref, do_ref, stats_ref, dqr_ref, dq_ref, acc_ref,
    *, near, bsize, depth, scale
):
    f32 = jnp.float32
    bf16 = jnp.bfloat16
    nq = q_ref.shape[0]
    acc_ref[...] = jnp.zeros(acc_ref.shape, f32)
    kcols = pl.ds(0, depth)
    vcols = pl.ds(depth, depth)
    nt = (((1,), (1,)), ((), ()))

    def body(b, carry):
        q = q_ref[b]
        do = do_ref[b]
        ids_l = [lk_ref[b * near + i] for i in range(near)]
        keys = jnp.concatenate([kv_ref[i, :, kcols] for i in ids_l], axis=0)
        vals = jnp.concatenate([kv_ref[i, :, vcols] for i in ids_l], axis=0)
        q_s = q * scale
        do_s = do * scale
        stats = stats_ref[b]
        top = row_to_column(stats[0:1, :])
        rtot = row_to_column(stats[1:2, :])
        delta = row_to_column(stats[2:3, :])
        s = lax.dot_general(q_s, keys, nt, preferred_element_type=f32)
        w = (jnp.exp(s - top) * rtot).astype(bf16)
        dw = lax.dot_general(do_s, vals, nt, preferred_element_type=f32)
        ds = (w.astype(f32) * (dw - delta)).astype(bf16)
        dq = dqr_ref[b] + jnp.dot(ds, keys, preferred_element_type=f32)
        dq_ref[b] = dq.astype(bf16)
        dk_t = jnp.dot(q.T, ds, preferred_element_type=f32)
        dv_t = jnp.dot(do.T, w, preferred_element_type=f32)
        dkv_t = jnp.concatenate([dk_t, dv_t], axis=0)
        for i in range(near):
            part = dkv_t[:, i * bsize:(i + 1) * bsize]
            acc_ref[ids_l[i]] = acc_ref[ids_l[i]] + part
        return carry

    lax.fori_loop(0, nq, body, 0, unroll=4)


def fused_attention(local_ids, remote_ids, q, kv, d_out, pool, bias, scale):
    nq, bsize, depth = d_out.shape
    near = local_ids.size // nq
    far = remote_ids.size // nq
    npool = pool.shape[0]
    f32 = jnp.float32
    smem = pl.BlockSpec(memory_space=pltpu.SMEM)
    vmem = pl.BlockSpec(memory_space=pltpu.VMEM)
    kv_t = (2 * depth, bsize)
    params = pltpu.CompilerParams(vmem_limit_bytes=60 * 1024 * 1024)
    per_step = 8
    blk = lambda *shape: pl.BlockSpec((per_step,) + shape, lambda i: (i,) + (0,) * len(shape))
    whole = lambda a: pl.BlockSpec(a.shape, lambda i: (0,) * a.ndim)
    o, dq_r, stats, slot = pl.pallas_call(
        lambda *refs: remote_kernel(
            *refs, near=near, far=far, bsize=bsize, depth=depth, scale=scale
        ),
        grid=(nq // per_step,),
        out_shape=(
            jax.ShapeDtypeStruct((nq, bsize, depth), jnp.bfloat16),
            jax.ShapeDtypeStruct((nq, bsize, depth), f32),
            jax.ShapeDtypeStruct((nq, 3, bsize), f32),
            jax.ShapeDtypeStruct((npool,) + kv_t, jnp.bfloat16),
        ),
        in_specs=[
            smem, smem, blk(bsize, depth), whole(kv), blk(bsize, depth), whole(pool),
            pl.BlockSpec((per_step, bias.shape[1]), lambda i: (i, 0)),
        ],
        out_specs=(
            blk(bsize, depth), blk(bsize, depth), blk(3, bsize),
            pl.BlockSpec((npool,) + kv_t, lambda i: (0, 0, 0)),
        ),
        scratch_shapes=[pltpu.VMEM((npool,) + kv_t, f32)],
        compiler_params=pltpu.CompilerParams(
            dimension_semantics=("arbitrary",), vmem_limit_bytes=60 * 1024 * 1024
        ),
    )(local_ids, remote_ids, q, kv, d_out, pool, bias)
    dq, acc = pl.pallas_call(
        lambda *refs: local_kernel(*refs, near=near, bsize=bsize, depth=depth, scale=scale),
        out_shape=(
            jax.ShapeDtypeStruct((nq, bsize, depth), jnp.bfloat16),
            jax.ShapeDtypeStruct((nq,) + kv_t, f32),
        ),
        in_specs=[smem] + [vmem] * 5,
        out_specs=(vmem, vmem),
        compiler_params=params,
    )(local_ids, q, kv, d_out, stats, dq_r)
    return o, dq, acc, slot


def finish_kernel(ids_ref, acc_ref, ret_ref, out_ref, total_ref):
    step = pl.program_id(0)
    chunk = ret_ref.shape[0]

    @pl.when(step == 0)
    def _():
        total_ref[...] = acc_ref[...]

    def add_slot(j, carry):
        i = ids_ref[step * chunk + j]
        total_ref[i] = total_ref[i] + ret_ref[j].astype(jnp.float32)
        return carry

    lax.fori_loop(0, chunk, add_slot, 0, unroll=8)

    def emit(b, carry):
        out_ref[b] = total_ref[b].T.astype(jnp.bfloat16)
        return carry

    @pl.when(step == pl.num_programs(0) - 1)
    def _():
        lax.fori_loop(0, acc_ref.shape[0], emit, 0, unroll=4)


def finish_grads(send_ids, acc, returned):
    nq, kvw, bsize = acc.shape
    steps = 4
    chunk = returned.shape[0] // steps
    smem = pl.BlockSpec(memory_space=pltpu.SMEM)
    return pl.pallas_call(
        finish_kernel,
        grid=(steps,),
        out_shape=jax.ShapeDtypeStruct((nq, bsize, kvw), jnp.bfloat16),
        in_specs=[
            smem,
            pl.BlockSpec(acc.shape, lambda i: (0, 0, 0)),
            pl.BlockSpec((chunk,) + returned.shape[1:], lambda i: (i, 0, 0)),
        ],
        out_specs=pl.BlockSpec((nq, bsize, kvw), lambda i: (0, 0, 0)),
        scratch_shapes=[pltpu.VMEM(acc.shape, jnp.float32)],
        compiler_params=pltpu.CompilerParams(
            dimension_semantics=("arbitrary",), vmem_limit_bytes=60 * 1024 * 1024
        ),
    )(send_ids, acc, returned)


def head_exchange(x, axis):
    n = x.shape[0]
    me = lax.axis_index(axis)
    out = x
    for k in range(1, n):
        perm = [(i, (i + k) % n) for i in range(n)]
        part = lax.dynamic_index_in_dim(x, (me + k) % n, 0, keepdims=True)
        got = lax.ppermute(part, axis, perm)
        out = lax.dynamic_update_index_in_dim(out, got, (me + n - k) % n, 0)
    return out


def local(
    features,
    norm_gain,
    w_qkv,
    w_out,
    grad_y,
    local_keys,
    remote_keys,
    boundary_blocks,
    boundary_count,
):
    f32 = jnp.float32
    bf16 = jnp.bfloat16
    nhead = lax.axis_size("head")
    rows, width = features.shape
    per = HEADS // nhead
    depth = width // HEADS
    hwide = per * depth
    nblk, near_count = local_keys.shape
    far_count = remote_keys.shape[1]
    ndom = boundary_blocks.shape[1]
    pair_slots = boundary_blocks.shape[2]
    slots = ndom * pair_slots
    grows = rows * nhead
    bsize = grows // nblk
    score_scale = 1.0 / math.sqrt(depth)

    xf = features.astype(f32)
    inv = lax.rsqrt(jnp.mean(xf * xf, axis=1, keepdims=True) + EPS)
    normed = xf * inv
    hidden = (normed * norm_gain).astype(bf16)
    w_q = w_qkv[:, :width].reshape(width, nhead, hwide).transpose(1, 0, 2)
    w_kv = (
        w_qkv[:, width:]
        .reshape(width, 2, nhead, hwide)
        .transpose(2, 0, 1, 3)
        .reshape(nhead, width, 2 * hwide)
    )
    w_out_heads = w_out.reshape(nhead, hwide, width)
    kv_own = jnp.einsum("rd,hdc->hrc", hidden, w_kv, preferred_element_type=f32).astype(bf16)
    kv = lax.all_to_all(kv_own, "head", split_axis=0, concat_axis=0, tiled=True).reshape(
        nblk, bsize, 2 * hwide
    )
    q_own = jnp.einsum("rd,hdc->hrc", hidden, w_q, preferred_element_type=f32).astype(bf16)
    d_attn = jnp.einsum("rf,hef->hre", grad_y, w_out_heads, preferred_element_type=f32).astype(bf16)

    send_ids = boundary_blocks[0].reshape(slots)
    outgoing = jnp.take(kv, send_ids, axis=0, mode="clip")
    outgoing, q_own, d_attn = lax.optimization_barrier((outgoing, q_own, d_attn))
    queries = head_exchange(q_own, "head").reshape(nblk, bsize, hwide)
    d_group = head_exchange(d_attn, "head").reshape(nblk, bsize, hwide)
    pool = lax.all_to_all(
        outgoing.reshape(ndom, pair_slots * bsize, 2 * hwide),
        "dom",
        split_axis=0,
        concat_axis=0,
        tiled=True,
    ).reshape(slots, bsize, 2 * hwide)
    slot_alive = (jnp.arange(pair_slots, dtype=jnp.int32)[None, :] < boundary_count).reshape(slots)
    remote_alive = jnp.take(slot_alive, remote_keys, axis=0, mode="clip")
    bias_far = jnp.where(remote_alive, 0.0, -jnp.inf).astype(f32)
    bias = jnp.concatenate([jnp.zeros((nblk, near_count), f32), bias_far], axis=1)
    bias = jnp.repeat(bias, bsize, axis=1)

    o, d_q, acc, slot_grads = fused_attention(
        local_keys.reshape(-1), remote_keys.reshape(-1), queries, kv, d_group, pool, bias,
        score_scale,
    )

    attn = head_exchange(o.reshape(nhead, rows, hwide), "head")
    mixed_out = (
        xf + jnp.einsum("hre,hef->rf", attn, w_out_heads, preferred_element_type=f32)
    ).astype(bf16)
    d_rows_q = head_exchange(d_q.reshape(nhead, rows, hwide), "head")
    d_hidden_q = jnp.einsum("hrc,hdc->rd", d_rows_q, w_q, preferred_element_type=f32)

    returned = lax.all_to_all(
        slot_grads.reshape(ndom, pair_slots * 2 * hwide, bsize),
        "dom",
        split_axis=0,
        concat_axis=0,
        tiled=True,
    ).reshape(slots, 2 * hwide, bsize)
    d_kv = finish_grads(send_ids, acc, returned)
    d_rows = lax.all_to_all(
        d_kv.reshape(nhead, rows, 2 * hwide), "head", split_axis=0, concat_axis=0, tiled=True
    )
    d_hidden = d_hidden_q + jnp.einsum("hrc,hdc->rd", d_rows, w_kv, preferred_element_type=f32)
    d_normed = d_hidden * norm_gain
    d_input = inv * (d_normed - normed * jnp.mean(d_normed * normed, axis=1, keepdims=True))
    grad_x = (grad_y.astype(f32) + d_input).astype(bf16)
    return (mixed_out, grad_x)


def solution(mesh):
    return jax.shard_map(
        local,
        mesh=mesh,
        in_specs=(
            P(("dom", "head"), None),
            P(),
            P(),
            P(),
            P(("dom", "head"), None),
            P("dom", None),
            P("dom", None),
            P("dom", None, None),
            P(None, "dom"),
        ),
        out_specs=(P(("dom", "head"), None), P(("dom", "head"), None)),
        check_vma=False,
    )
```

```python
import math

import jax
import jax.numpy as jnp
from jax import lax
from jax.experimental import pallas as pl
from jax.experimental.pallas import tpu as pltpu
from jax.sharding import PartitionSpec as P

HEADS = 8
EPS = 1e-05


def load_blocks(kv_ref, pool_ref, ids_l, ids_r, cols):
    return jnp.concatenate(
        [kv_ref[i, :, cols] for i in ids_l] + [pool_ref[i, :, cols] for i in ids_r], axis=0
    )


def column_to_row(col):
    n = col.shape[0]
    return jnp.broadcast_to(col, (n, n)).T[0:1, :]


def row_to_column(row):
    n = row.shape[1]
    return jnp.broadcast_to(row, (n, n)).T[:, 0:1]


def remote_kernel(
    lk_ref, rk_ref, q_ref, kv_ref, do_ref, pool_ref, bias_ref, o_ref, dq_ref, stats_ref,
    slot_ref, slot_acc, *, near, far, bsize, depth, scale
):
    f32 = jnp.float32
    bf16 = jnp.bfloat16
    nq = q_ref.shape[0]
    step = pl.program_id(0)

    @pl.when(step == 0)
    def _():
        slot_acc[...] = jnp.zeros(slot_acc.shape, f32)

    kcols = pl.ds(0, depth)
    vcols = pl.ds(depth, depth)
    nt = (((1,), (1,)), ((), ()))
    split = near * bsize

    def body(b, carry):
        g = step * nq + b
        q = q_ref[b]
        do = do_ref[b]
        ids_l = [lk_ref[g * near + i] for i in range(near)]
        ids_r = [rk_ref[g * far + i] for i in range(far)]
        keys = load_blocks(kv_ref, pool_ref, ids_l, ids_r, kcols)
        vals = load_blocks(kv_ref, pool_ref, ids_l, ids_r, vcols)
        q_s = q * scale
        do_s = do * scale
        s = lax.dot_general(q_s, keys, nt, preferred_element_type=f32)
        s = s + bias_ref[pl.ds(b, 1), :]
        top = jnp.max(s, axis=1, keepdims=True)
        expo = jnp.exp(s - top)
        total = jnp.sum(expo, axis=1, keepdims=True)
        rtot = 1.0 / total
        w = (expo * rtot).astype(bf16)
        o = jnp.dot(w, vals, preferred_element_type=f32).astype(bf16)
        o_ref[b] = o
        delta = jnp.sum(do_s.astype(f32) * o.astype(f32), axis=1, keepdims=True)
        stats_ref[b] = jnp.concatenate(
            [column_to_row(top), column_to_row(rtot), column_to_row(delta)], axis=0
        )
        keys_r = keys[split:]
        vals_r = vals[split:]
        w_r = w[:, split:]
        dw = lax.dot_general(do_s, vals_r, nt, preferred_element_type=f32)
        ds = (w_r.astype(f32) * (dw - delta)).astype(bf16)
        dq_ref[b] = jnp.dot(ds, keys_r, preferred_element_type=f32)
        dk_t = jnp.dot(q.T, ds, preferred_element_type=f32)
        dv_t = jnp.dot(do.T, w_r, preferred_element_type=f32)
        dkv_t = jnp.concatenate([dk_t, dv_t], axis=0)
        for i in range(far):
            part = dkv_t[:, i * bsize:(i + 1) * bsize]
            slot_acc[ids_r[i]] = slot_acc[ids_r[i]] + part
        return carry

    lax.fori_loop(0, nq, body, 0, unroll=4)

    @pl.when(step == pl.num_programs(0) - 1)
    def _():
        slot_ref[...] = slot_acc[...].astype(bf16)


def local_kernel(
    lk_ref, q_ref, kv_ref, do_ref, stats_ref, dqr_ref, dq_ref, acc_ref,
    *, near, bsize, depth, scale
):
    f32 = jnp.float32
    bf16 = jnp.bfloat16
    nq = q_ref.shape[0]
    acc_ref[...] = jnp.zeros(acc_ref.shape, f32)
    kcols = pl.ds(0, depth)
    vcols = pl.ds(depth, depth)
    nt = (((1,), (1,)), ((), ()))

    def body(b, carry):
        q = q_ref[b]
        do = do_ref[b]
        ids_l = [lk_ref[b * near + i] for i in range(near)]
        keys = jnp.concatenate([kv_ref[i, :, kcols] for i in ids_l], axis=0)
        vals = jnp.concatenate([kv_ref[i, :, vcols] for i in ids_l], axis=0)
        q_s = q * scale
        do_s = do * scale
        stats = stats_ref[b]
        top = row_to_column(stats[0:1, :])
        rtot = row_to_column(stats[1:2, :])
        delta = row_to_column(stats[2:3, :])
        s = lax.dot_general(q_s, keys, nt, preferred_element_type=f32)
        w = (jnp.exp(s - top) * rtot).astype(bf16)
        dw = lax.dot_general(do_s, vals, nt, preferred_element_type=f32)
        ds = (w.astype(f32) * (dw - delta)).astype(bf16)
        dq = dqr_ref[b] + jnp.dot(ds, keys, preferred_element_type=f32)
        dq_ref[b] = dq.astype(bf16)
        dk_t = jnp.dot(q.T, ds, preferred_element_type=f32)
        dv_t = jnp.dot(do.T, w, preferred_element_type=f32)
        dkv_t = jnp.concatenate([dk_t, dv_t], axis=0)
        for i in range(near):
            part = dkv_t[:, i * bsize:(i + 1) * bsize]
            acc_ref[ids_l[i]] = acc_ref[ids_l[i]] + part
        return carry

    lax.fori_loop(0, nq, body, 0, unroll=4)


def fused_attention(local_ids, remote_ids, q, kv, d_out, pool, bias, scale):
    nq, bsize, depth = d_out.shape
    near = local_ids.size // nq
    far = remote_ids.size // nq
    npool = pool.shape[0]
    f32 = jnp.float32
    smem = pl.BlockSpec(memory_space=pltpu.SMEM)
    vmem = pl.BlockSpec(memory_space=pltpu.VMEM)
    kv_t = (2 * depth, bsize)
    params = pltpu.CompilerParams(vmem_limit_bytes=60 * 1024 * 1024)
    per_step = 8
    blk = lambda *shape: pl.BlockSpec((per_step,) + shape, lambda i: (i,) + (0,) * len(shape))
    whole = lambda a: pl.BlockSpec(a.shape, lambda i: (0,) * a.ndim)
    o, dq_r, stats, slot = pl.pallas_call(
        lambda *refs: remote_kernel(
            *refs, near=near, far=far, bsize=bsize, depth=depth, scale=scale
        ),
        grid=(nq // per_step,),
        out_shape=(
            jax.ShapeDtypeStruct((nq, bsize, depth), jnp.bfloat16),
            jax.ShapeDtypeStruct((nq, bsize, depth), f32),
            jax.ShapeDtypeStruct((nq, 3, bsize), f32),
            jax.ShapeDtypeStruct((npool,) + kv_t, jnp.bfloat16),
        ),
        in_specs=[
            smem, smem, blk(bsize, depth), whole(kv), blk(bsize, depth), whole(pool),
            pl.BlockSpec((per_step, bias.shape[1]), lambda i: (i, 0)),
        ],
        out_specs=(
            blk(bsize, depth), blk(bsize, depth), blk(3, bsize),
            pl.BlockSpec((npool,) + kv_t, lambda i: (0, 0, 0)),
        ),
        scratch_shapes=[pltpu.VMEM((npool,) + kv_t, f32)],
        compiler_params=pltpu.CompilerParams(
            dimension_semantics=("arbitrary",), vmem_limit_bytes=60 * 1024 * 1024
        ),
    )(local_ids, remote_ids, q, kv, d_out, pool, bias)
    dq, acc = pl.pallas_call(
        lambda *refs: local_kernel(*refs, near=near, bsize=bsize, depth=depth, scale=scale),
        out_shape=(
            jax.ShapeDtypeStruct((nq, bsize, depth), jnp.bfloat16),
            jax.ShapeDtypeStruct((nq,) + kv_t, f32),
        ),
        in_specs=[smem] + [vmem] * 5,
        out_specs=(vmem, vmem),
        compiler_params=params,
    )(local_ids, q, kv, d_out, stats, dq_r)
    return o, dq, acc, slot


def finish_kernel(ids_ref, acc_ref, ret_ref, out_ref, total_ref):
    total_ref[...] = acc_ref[...]

    def add_slot(j, carry):
        i = ids_ref[j]
        total_ref[i] = total_ref[i] + ret_ref[j].astype(jnp.float32)
        return carry

    lax.fori_loop(0, ret_ref.shape[0], add_slot, 0, unroll=16)

    def emit(b, carry):
        out_ref[b] = total_ref[b].T.astype(jnp.bfloat16)
        return carry

    lax.fori_loop(0, acc_ref.shape[0], emit, 0, unroll=8)


def finish_grads(send_ids, acc, returned):
    nq, kvw, bsize = acc.shape
    smem = pl.BlockSpec(memory_space=pltpu.SMEM)
    vmem = pl.BlockSpec(memory_space=pltpu.VMEM)
    return pl.pallas_call(
        finish_kernel,
        out_shape=jax.ShapeDtypeStruct((nq, bsize, kvw), jnp.bfloat16),
        in_specs=[smem, vmem, vmem],
        out_specs=vmem,
        scratch_shapes=[pltpu.VMEM(acc.shape, jnp.float32)],
        compiler_params=pltpu.CompilerParams(vmem_limit_bytes=60 * 1024 * 1024),
    )(send_ids, acc, returned)


def head_exchange(x, axis):
    n = x.shape[0]
    me = lax.axis_index(axis)
    out = x
    for k in range(1, n):
        perm = [(i, (i + k) % n) for i in range(n)]
        part = lax.dynamic_index_in_dim(x, (me + k) % n, 0, keepdims=True)
        got = lax.ppermute(part, axis, perm)
        out = lax.dynamic_update_index_in_dim(out, got, (me + n - k) % n, 0)
    return out


def local(
    features,
    norm_gain,
    w_qkv,
    w_out,
    grad_y,
    local_keys,
    remote_keys,
    boundary_blocks,
    boundary_count,
):
    f32 = jnp.float32
    bf16 = jnp.bfloat16
    nhead = lax.axis_size("head")
    rows, width = features.shape
    per = HEADS // nhead
    depth = width // HEADS
    hwide = per * depth
    nblk, near_count = local_keys.shape
    far_count = remote_keys.shape[1]
    ndom = boundary_blocks.shape[1]
    pair_slots = boundary_blocks.shape[2]
    slots = ndom * pair_slots
    grows = rows * nhead
    bsize = grows // nblk
    score_scale = 1.0 / math.sqrt(depth)

    xf = features.astype(f32)
    inv = lax.rsqrt(jnp.mean(xf * xf, axis=1, keepdims=True) + EPS)
    normed = xf * inv
    hidden = (normed * norm_gain).astype(bf16)
    w_q = w_qkv[:, :width].reshape(width, nhead, hwide).transpose(1, 0, 2)
    w_kv = (
        w_qkv[:, width:]
        .reshape(width, 2, nhead, hwide)
        .transpose(2, 0, 1, 3)
        .reshape(nhead, width, 2 * hwide)
    )
    w_out_heads = w_out.reshape(nhead, hwide, width)
    kv_own = jnp.einsum("rd,hdc->hrc", hidden, w_kv, preferred_element_type=f32).astype(bf16)
    kv = lax.all_to_all(kv_own, "head", split_axis=0, concat_axis=0, tiled=True).reshape(
        nblk, bsize, 2 * hwide
    )
    q_own = jnp.einsum("rd,hdc->hrc", hidden, w_q, preferred_element_type=f32).astype(bf16)
    d_attn = jnp.einsum("rf,hef->hre", grad_y, w_out_heads, preferred_element_type=f32).astype(bf16)

    send_ids = boundary_blocks[0].reshape(slots)
    outgoing = jnp.take(kv, send_ids, axis=0, mode="clip")
    outgoing, q_own, d_attn = lax.optimization_barrier((outgoing, q_own, d_attn))
    queries = head_exchange(q_own, "head").reshape(nblk, bsize, hwide)
    d_group = head_exchange(d_attn, "head").reshape(nblk, bsize, hwide)
    pool = lax.all_to_all(
        outgoing.reshape(ndom, pair_slots * bsize, 2 * hwide),
        "dom",
        split_axis=0,
        concat_axis=0,
        tiled=True,
    ).reshape(slots, bsize, 2 * hwide)
    slot_alive = (jnp.arange(pair_slots, dtype=jnp.int32)[None, :] < boundary_count).reshape(slots)
    remote_alive = jnp.take(slot_alive, remote_keys, axis=0, mode="clip")
    bias_far = jnp.where(remote_alive, 0.0, -jnp.inf).astype(f32)
    bias = jnp.concatenate([jnp.zeros((nblk, near_count), f32), bias_far], axis=1)
    bias = jnp.repeat(bias, bsize, axis=1)

    o, d_q, acc, slot_grads = fused_attention(
        local_keys.reshape(-1), remote_keys.reshape(-1), queries, kv, d_group, pool, bias,
        score_scale,
    )

    attn = head_exchange(o.reshape(nhead, rows, hwide), "head")
    mixed_out = (
        xf + jnp.einsum("hre,hef->rf", attn, w_out_heads, preferred_element_type=f32)
    ).astype(bf16)
    d_rows_q = head_exchange(d_q.reshape(nhead, rows, hwide), "head")
    d_hidden_q = jnp.einsum("hrc,hdc->rd", d_rows_q, w_q, preferred_element_type=f32)

    returned = lax.all_to_all(
        slot_grads.reshape(ndom, pair_slots * 2 * hwide, bsize),
        "dom",
        split_axis=0,
        concat_axis=0,
        tiled=True,
    ).reshape(slots, 2 * hwide, bsize)
    d_kv = finish_grads(send_ids, acc, returned)
    d_rows = lax.all_to_all(
        d_kv.reshape(nhead, rows, 2 * hwide), "head", split_axis=0, concat_axis=0, tiled=True
    )
    d_hidden = d_hidden_q + jnp.einsum("hrc,hdc->rd", d_rows, w_kv, preferred_element_type=f32)
    d_normed = d_hidden * norm_gain
    d_input = inv * (d_normed - normed * jnp.mean(d_normed * normed, axis=1, keepdims=True))
    grad_x = (grad_y.astype(f32) + d_input).astype(bf16)
    return (mixed_out, grad_x)


def solution(mesh):
    return jax.shard_map(
        local,
        mesh=mesh,
        in_specs=(
            P(("dom", "head"), None),
            P(),
            P(),
            P(),
            P(("dom", "head"), None),
            P("dom", None),
            P("dom", None),
            P("dom", None, None),
            P(None, "dom"),
        ),
        out_specs=(P(("dom", "head"), None), P(("dom", "head"), None)),
        check_vma=False,
    )
```
